256 devices in a mesh: sta: 64 (over z, y, core), tm: 4 (over x).
Axes of the slice: x: 4, y: 4, z: 8, core: 2. Of those that a mesh axis runs over, the one named last changes fastest.
Arguments:
- records: bfloat16 [4096, 8192], P('sta', 'tm'), may hold values from -6 to 6
- band_taps: bfloat16 [1024], replicated, may hold values from -0.1875 to 0.1875
- station_owners: int32 [4096, 2], P('sta'), may hold values from 0 to 63, all different within a row; in each aligned block of 64 rows (0 to 63, 64 to 127, ...) at most 4 rows name the same one
Outputs:
- correlations: bfloat16 [4096, 2, 64, 2, 512], P('sta', None, None, None, 'tm')
The draws below stay inside these ranges and needn't reach their ends.
Inputs may be any that keep to these rules, and one draw needn't show every extreme that they name: `station_owners`: each row names 2 different station blocks. Within the rows of one station block (64 aligned rows) no block is named by more than 4 rows, and some block is named by exactly 4 rows.
All inputs are finite; a program needn't handle non-finite values.
Results may differ from the reference program's by a relative error of at most 0.0069.
Values may be sent and summed in bfloat16 or wider, within the bound.
No kernel may reach another device: no remote copies, remote signals or barrier semaphores. Data moves between devices by JAX's collectives and lax.ppermute only.
A program may use at most 128 MiB of HBM per device.

```python
import math
import jax
import jax.numpy as jnp
import numpy as np
from jax import lax

WIN = 1024
TAPS = 1024
FREQ = 512
SMOOTH = 64
NW = 8
SB = 64
TOPK = 2
STATIONS = 4096
CAP = 4
N_STA = 64


def block_scale(key, extent, cuts, smallest, high):
    factor_of = 1.0
    for position, parts in cuts:
        steps = jax.random.uniform(jax.random.fold_in(jax.random.fold_in(key, 6), position), (parts,), jnp.float32, smallest / len(cuts), high / len(cuts))
        factor_of = factor_of * jnp.repeat(jnp.exp(steps), extent[position] // parts).reshape((-1,) + (1,) * (len(extent) - 1 - position))
    return factor_of


def deal_out(own_key, own, number, rows, number_of, top, reach, skew):
    order = jax.random.permutation(own_key, number_of)
    packed, usual = shares(number_of, rows * top, reach, skew, True), shares(number_of, rows * top, reach, skew, False)
    places = jnp.arange(number_of)

    def named(sizes, turn):
        used = int((sizes > 0).sum())
        fixed = max(1, used // 4)
        shifted = fixed + (places - fixed + turn * (used - fixed)) % max(1, number_of - fixed)
        return jnp.zeros((number_of,), jnp.int32).at[order[jnp.where(places < fixed, places, shifted)]].set(jnp.asarray(sizes, jnp.int32))

    sizes = jnp.where(number % 4 == 0, named(packed, number // 4), named(usual, number - number // 4 - 1))
    mixed = jax.random.permutation(jax.random.fold_in(own, 3), number_of)
    giver, taker = mixed[0:number_of // 2 * 2:2], mixed[1:number_of // 2 * 2:2]
    slack = jnp.minimum(sizes[giver] - 1, reach - sizes[taker]) // 2
    slack = jnp.where((giver == order[0]) | (taker == order[0]) | (sizes[taker] == 0), 0, jnp.maximum(slack, 0))
    shifted = jax.random.randint(jax.random.fold_in(own, 4), (number_of // 2,), 0, 1 << 20) % (slack + 1)
    sizes = sizes.at[giver].add(-shifted).at[taker].add(shifted)
    items = jnp.searchsorted(jnp.cumsum(sizes), jnp.arange(rows * top), side="right").astype(jnp.int32)
    table = items.reshape(top, rows).T
    table = table[jax.random.permutation(jax.random.fold_in(own, 1), rows)]
    turn = jax.random.randint(jax.random.fold_in(own, 2), (rows, 1), 0, top)
    return jnp.take_along_axis(table, (jnp.arange(top)[None, :] + turn) % top, axis=1)


def shares(count, total, limit, lean, full):
    loads = [(1 << 20) // math.isqrt(standing ** lean) + 1 for standing in range(1, count + 1)]
    largest = limit if full else min(limit, max(-(-total // count), total * loads[0] // sum(loads)))
    least = 1 if total - largest >= count - 1 else 0
    holding, surplus = [largest] + [least] * (count - 1), total - largest - least * (count - 1)
    while surplus > 0:
        candidates = [i for i in range(1, count) if holding[i] < largest] or [i for i in range(1, count) if holding[i] < limit]
        mass, budget = sum([loads[i] for i in candidates]), surplus
        for i in candidates:
            addition = min(limit - holding[i], max(1, budget * loads[i] // mass), surplus)
            holding[i] = holding[i] + addition
            surplus = surplus - addition
    return np.array(holding)


def gaussian(key, dims, deviation, reach, cuts=(), kind=jnp.bfloat16):
    entries = deviation * jax.random.normal(key, dims, jnp.float32)
    if cuts:
        entries = entries * block_scale(key, dims, cuts, -0.22, 0.18)
    return jnp.clip(entries, -reach, reach).astype(kind)


def setup_inputs(seed: int = 0) -> dict:
    streams_of = jax.random.split(jax.random.key(seed), 4)
    records = gaussian(streams_of[0], (STATIONS, NW * WIN), 1.0, 6.0, ((0, 64), (1, 4)))
    band_taps = gaussian(streams_of[1], (TAPS,), TAPS ** -0.5, 0.1875)
    station_owners_keys = jax.random.split(jax.random.fold_in(streams_of[2], 1), STATIONS // SB)
    station_owners_turns = jax.random.permutation(jax.random.fold_in(streams_of[2], 3), STATIONS // SB)
    station_owners = jax.vmap(lambda own, number: deal_out(jax.random.fold_in(streams_of[2], 2), own, number, SB, N_STA, TOPK, CAP, 2))(station_owners_keys, station_owners_turns).reshape((STATIONS, TOPK))
    return dict(records=records, band_taps=band_taps, station_owners=station_owners)


def filter_matrices(band_taps):
    taps_len = band_taps.shape[0]
    column = jnp.arange(taps_len, dtype=jnp.int32)
    lag_value = column[None, :] - column[:, None]
    zero_tap = jnp.zeros((), band_taps.dtype)
    lower_part = jnp.where(lag_value >= 0, band_taps[jnp.clip(lag_value, 0, taps_len - 1)], zero_tap)
    upper_part = jnp.where(lag_value < 0, band_taps[jnp.clip(lag_value + taps_len, 0, taps_len - 1)], zero_tap)
    return (lower_part, upper_part)

def transform_table(window_len):
    bin_count = window_len // 2
    sample_index = jnp.arange(window_len, dtype=jnp.int32)[:, None]
    bin_index = jnp.arange(bin_count, dtype=jnp.int32)[None, :]
    phase_angle = (sample_index * bin_index % window_len).astype(jnp.float32) * (2.0 * math.pi / window_len)
    return jnp.concatenate([jnp.cos(phase_angle), -jnp.sin(phase_angle)], axis=1).astype(jnp.bfloat16)

def band_matrix(bin_count, smooth_len):
    bin_index = jnp.arange(bin_count, dtype=jnp.int32)
    offsets = (bin_index[:, None] - bin_index[None, :]) % bin_count
    half_span = smooth_len // 2
    inside = (offsets < half_span) | (offsets >= bin_count - half_span)
    return inside.astype(jnp.float32)

def whiten(record_rows, band_taps):
    station_count = record_rows.shape[0]
    series = record_rows.reshape(station_count, NW, WIN)
    earlier = jnp.concatenate([jnp.zeros_like(series[:, :1]), series[:, :-1]], axis=1)
    lower_part, upper_part = filter_matrices(band_taps)
    filtered = jnp.dot(series.reshape(-1, WIN), lower_part, preferred_element_type=jnp.float32)
    filtered = filtered + jnp.dot(earlier.reshape(-1, WIN), upper_part, preferred_element_type=jnp.float32)
    filtered = filtered.astype(jnp.bfloat16)
    spectrum = jnp.dot(filtered, transform_table(WIN), preferred_element_type=jnp.float32)
    real_part = spectrum[:, :FREQ]
    imag_part = spectrum[:, FREQ:]
    power_sum = real_part * real_part + imag_part * imag_part
    smooth = jnp.dot(power_sum, band_matrix(FREQ, SMOOTH), precision=lax.Precision.HIGHEST, preferred_element_type=jnp.float32) / SMOOTH
    whiten_scale = lax.rsqrt(smooth + 1e-05)
    whitened = (spectrum.reshape(-1, 2, FREQ) * whiten_scale[:, None, :]).astype(jnp.bfloat16)
    return whitened.reshape(station_count, NW, 2, FREQ)

def reference(records, band_taps, station_owners):
    whitened = whiten(records, band_taps)
    blocks_all = whitened.reshape(N_STA, SB, NW, 2, FREQ)
    owner_rows = station_owners.reshape(N_STA, SB, TOPK)

    def per_block(block_item):
        own_block, named = block_item
        partners = blocks_all[named].astype(jnp.float32)
        signal = own_block.astype(jnp.float32)
        sig_re = signal[:, None, None, :, 0]
        sig_im = signal[:, None, None, :, 1]
        par_re = partners[..., 0, :]
        par_im = partners[..., 1, :]
        real_sum = lax.optimization_barrier(jnp.sum(par_re * sig_re + par_im * sig_im, axis=3))
        imag_sum = lax.optimization_barrier(jnp.sum(par_re * sig_im - par_im * sig_re, axis=3))
        return jnp.stack([real_sum, imag_sum], axis=3)
    stacked = lax.map(per_block, (blocks_all, owner_rows))
    return stacked.reshape(STATIONS, TOPK, SB, 2, FREQ).astype(jnp.bfloat16)
```

```python
import math

import jax
import jax.numpy as jnp
from jax import lax
from jax.experimental import pallas as pl
from jax.experimental.pallas import tpu as pltpu
from jax.sharding import Mesh
from jax.sharding import PartitionSpec as P

WIN = 1024
FREQ = 512
SMOOTH = 64
NW = 8
CORES = 2


def toeplitz_kernel(seed_ref, out_ref):
    rows = 128
    base = jnp.broadcast_to(seed_ref[...], (rows, seed_ref.shape[1]))
    for blk in range(out_ref.shape[0] // rows):
        rolled = pltpu.roll(base, blk * rows, 1, stride=1, stride_axis=0)
        out_ref[blk * rows : (blk + 1) * rows, :] = rolled.astype(out_ref.dtype)


def toeplitz_both(band_taps):
    taps_len = band_taps.shape[0]
    seed = jnp.concatenate(
        [band_taps.astype(jnp.float32), jnp.zeros((taps_len,), jnp.float32)]
    )[None, :]
    return pl.pallas_call(
        toeplitz_kernel,
        out_shape=jax.ShapeDtypeStruct((taps_len, 2 * taps_len), jnp.bfloat16),
    )(seed)


def transform_table(window_len):
    bin_count = window_len // 2
    sample_index = jnp.arange(window_len, dtype=jnp.int32)[:, None]
    bin_index = jnp.arange(bin_count, dtype=jnp.int32)[None, :]
    phase_angle = (sample_index * bin_index % window_len).astype(jnp.float32) * (
        2.0 * math.pi / window_len
    )
    return jnp.concatenate([jnp.cos(phase_angle), -jnp.sin(phase_angle)], axis=1).astype(
        jnp.bfloat16
    )


def band_matrix(bin_count, smooth_len):
    bin_index = jnp.arange(bin_count, dtype=jnp.int32)
    offsets = (bin_index[:, None] - bin_index[None, :]) % bin_count
    half_span = smooth_len // 2
    inside = (offsets < half_span) | (offsets >= bin_count - half_span)
    return inside.astype(jnp.float32)


def shards(records, band_taps, station_owners):
    relayed = lax.all_to_all(records, "tm", split_axis=0, concat_axis=1, tiled=True)
    station_count = relayed.shape[0]
    both_parts = toeplitz_both(band_taps)
    series = relayed.reshape(station_count * NW, WIN)
    halves = jnp.dot(series, both_parts, preferred_element_type=jnp.float32)
    halves = halves.reshape(station_count, NW, 2 * WIN)
    carried = jnp.concatenate(
        [jnp.zeros_like(halves[:, :1, WIN:]), halves[:, :-1, WIN:]], axis=1
    )
    filtered = (halves[:, :, :WIN] + carried).astype(jnp.bfloat16).reshape(-1, WIN)
    spectrum = jnp.dot(filtered, transform_table(WIN), preferred_element_type=jnp.float32)
    real_part = spectrum[:, :FREQ]
    imag_part = spectrum[:, FREQ:]
    power_sum = real_part * real_part + imag_part * imag_part
    smooth = (
        jnp.dot(
            power_sum,
            band_matrix(FREQ, SMOOTH),
            precision=lax.Precision.HIGHEST,
            preferred_element_type=jnp.float32,
        )
        / SMOOTH
    )
    whiten_scale = lax.rsqrt(smooth + 1e-05)
    whitened = (spectrum.reshape(-1, 2, FREQ) * whiten_scale[:, None, :]).astype(jnp.bfloat16)
    whitened = whitened.reshape(station_count, NW, 2, FREQ)
    regrouped = lax.all_to_all(whitened, "tm", split_axis=3, concat_axis=0, tiled=True)
    own_count = regrouped.shape[0]
    same_core = lax.all_gather(regrouped, "zy", axis=0, tiled=False)
    both_cores = lax.all_gather(same_core, "c", axis=0, tiled=False)
    needed = both_cores[station_owners % CORES, station_owners // CORES]

    def block_sum(left_part, right_part):
        return jnp.einsum(
            "swf,skjwf->skjf", left_part, right_part, preferred_element_type=jnp.float32
        )

    sig_re = regrouped[:, :, 0]
    sig_im = regrouped[:, :, 1]
    par_re = needed[..., 0, :]
    par_im = needed[..., 1, :]
    real_sum = block_sum(sig_re, par_re) + block_sum(sig_im, par_im)
    imag_sum = block_sum(sig_im, par_re) - block_sum(sig_re, par_im)
    result = jnp.stack([real_sum, imag_sum], axis=3).astype(jnp.bfloat16)
    return result


def solution(mesh):
    n_sta, n_tm = mesh.shape["sta"], mesh.shape["tm"]
    split_mesh = Mesh(
        mesh.devices.reshape(n_sta // CORES, CORES, n_tm), ("zy", "c", "tm")
    )
    sta = ("zy", "c")
    placed = (P(sta, "tm"), P(), P(sta, None))
    return jax.shard_map(
        shards,
        mesh=split_mesh,
        in_specs=placed,
        out_specs=P(sta, None, None, None, "tm"),
        check_vma=False,
    )
```

```python
import math

import jax
import jax.numpy as jnp
from jax import lax
from jax.experimental import pallas as pl
from jax.experimental.pallas import tpu as pltpu
from jax.sharding import PartitionSpec as P

WIN = 1024
FREQ = 512
SMOOTH = 64
NW = 8
CORES = 2


def toeplitz_kernel(seed_ref, out_ref):
    rows = 128
    base = jnp.broadcast_to(seed_ref[...], (rows, seed_ref.shape[1]))
    for blk in range(out_ref.shape[0] // rows):
        rolled = pltpu.roll(base, blk * rows, 1, stride=1, stride_axis=0)
        out_ref[blk * rows : (blk + 1) * rows, :] = rolled.astype(out_ref.dtype)


def toeplitz_both(band_taps):
    taps_len = band_taps.shape[0]
    seed = jnp.concatenate(
        [band_taps.astype(jnp.float32), jnp.zeros((taps_len,), jnp.float32)]
    )[None, :]
    return pl.pallas_call(
        toeplitz_kernel,
        out_shape=jax.ShapeDtypeStruct((taps_len, 2 * taps_len), jnp.bfloat16),
    )(seed)


def transform_table(window_len):
    bin_count = window_len // 2
    sample_index = jnp.arange(window_len, dtype=jnp.int32)[:, None]
    bin_index = jnp.arange(bin_count, dtype=jnp.int32)[None, :]
    phase_angle = (sample_index * bin_index % window_len).astype(jnp.float32) * (
        2.0 * math.pi / window_len
    )
    return jnp.concatenate([jnp.cos(phase_angle), -jnp.sin(phase_angle)], axis=1).astype(
        jnp.bfloat16
    )


def band_matrix(bin_count, smooth_len):
    bin_index = jnp.arange(bin_count, dtype=jnp.int32)
    offsets = (bin_index[:, None] - bin_index[None, :]) % bin_count
    half_span = smooth_len // 2
    inside = (offsets < half_span) | (offsets >= bin_count - half_span)
    return inside.astype(jnp.float32)


ROWS = 32


def corr_kernel(owner_ref, part_ref, own_ref, out_hbm, scr, sem):
    rows_all, freq = part_ref.shape[2], part_ref.shape[3]
    n_pairs = owner_ref.shape[0]
    n_top = out_hbm.shape[1]
    chunk = min(ROWS, rows_all)
    row_id = lax.broadcasted_iota(jnp.int32, (chunk, freq), 0)
    even = (row_id % 2) == 0
    sign = jnp.where(even, 1.0, -1.0).astype(jnp.float32)

    def one(i, carry):
        slot = i % 2
        s = i // n_top
        k = i % n_top
        b = owner_ref[i]

        @pl.when(i >= 2)
        def _():
            pltpu.make_async_copy(scr.at[slot], out_hbm.at[0, 0], sem.at[slot]).wait()

        for c0 in range(0, rows_all, chunk):
            acc1 = jnp.zeros((chunk, freq), jnp.float32)
            acc2 = jnp.zeros((chunk, freq), jnp.float32)
            for w in range(NW):
                q = part_ref[b, w, c0 : c0 + chunk, :].astype(jnp.float32)
                sre = own_ref[s, 2 * w : 2 * w + 1, :].astype(jnp.float32)
                sim = own_ref[s, 2 * w + 1 : 2 * w + 2, :].astype(jnp.float32)
                acc1 = acc1 + q * sre
                acc2 = acc2 + q * sim
            up = pltpu.roll(acc2, chunk - 1, 0)
            dn = pltpu.roll(acc2, 1, 0)
            res = sign * acc1 + jnp.where(even, up, dn)
            scr[slot, c0 : c0 + chunk, :] = res.astype(scr.dtype)
        pltpu.make_async_copy(scr.at[slot], out_hbm.at[s, k], sem.at[slot]).start()
        return carry

    lax.fori_loop(0, n_pairs, one, 0)
    for back in range(min(2, n_pairs)):
        last = n_pairs - 1 - back
        pltpu.make_async_copy(scr.at[last % 2], out_hbm.at[0, 0], sem.at[last % 2]).wait()


def correlate(owners, part, own, out_shape):
    rows, freq = part.shape[2], part.shape[3]
    return pl.pallas_call(
        corr_kernel,
        out_shape=jax.ShapeDtypeStruct(out_shape, jnp.bfloat16),
        in_specs=[
            pl.BlockSpec(memory_space=pltpu.SMEM),
            pl.BlockSpec(memory_space=pltpu.VMEM),
            pl.BlockSpec(memory_space=pltpu.VMEM),
        ],
        out_specs=pl.BlockSpec(memory_space=pl.ANY),
        scratch_shapes=[pltpu.VMEM((2, rows, freq), jnp.bfloat16), pltpu.SemaphoreType.DMA((2,))],
        compiler_params=pltpu.CompilerParams(vmem_limit_bytes=48 * 1024 * 1024),
    )(owners, part, own)


def shards(records, band_taps, station_owners):
    relayed = lax.all_to_all(records, "tm", split_axis=0, concat_axis=1, tiled=True)
    station_count = relayed.shape[0]
    both_parts = toeplitz_both(band_taps)
    series = relayed.reshape(station_count * NW, WIN)
    halves = jnp.dot(series, both_parts, preferred_element_type=jnp.float32)
    halves = halves.reshape(station_count, NW, 2 * WIN)
    carried = jnp.concatenate(
        [jnp.zeros_like(halves[:, :1, WIN:]), halves[:, :-1, WIN:]], axis=1
    )
    filtered = (halves[:, :, :WIN] + carried).astype(jnp.bfloat16).reshape(-1, WIN)
    spectrum = jnp.dot(filtered, transform_table(WIN), preferred_element_type=jnp.float32)
    real_part = spectrum[:, :FREQ]
    imag_part = spectrum[:, FREQ:]
    power_sum = real_part * real_part + imag_part * imag_part
    smooth = (
        jnp.dot(
            power_sum,
            band_matrix(FREQ, SMOOTH),
            precision=lax.Precision.HIGHEST,
            preferred_element_type=jnp.float32,
        )
        / SMOOTH
    )
    whiten_scale = lax.rsqrt(smooth + 1e-05)
    whitened = (spectrum.reshape(-1, 2, FREQ) * whiten_scale[:, None, :]).astype(jnp.bfloat16)
    whitened = whitened.reshape(station_count, NW, 2, FREQ)
    regrouped = lax.all_to_all(whitened, "tm", split_axis=3, concat_axis=0, tiled=True)
    own_count = regrouped.shape[0]
    freq = regrouped.shape[3]
    contribution = regrouped.transpose(1, 0, 2, 3).reshape(NW, own_count * 2, freq)
    gathered = lax.all_gather(contribution, "sta", axis=0, tiled=False)
    own = regrouped.reshape(own_count, NW * 2, freq)
    out_shape = (own_count, station_owners.shape[1], own_count * 2, freq)
    result = correlate(station_owners.reshape(-1), gathered, own, out_shape)
    return result.reshape(own_count, station_owners.shape[1], own_count, 2, freq)


def solution(mesh):
    placed = (P("sta", "tm"), P(), P("sta", None))
    return jax.shard_map(
        shards,
        mesh=mesh,
        in_specs=placed,
        out_specs=P("sta", None, None, None, "tm"),
        check_vma=False,
    )
```

```python
import functools
import math

import jax
import jax.numpy as jnp
from jax import lax
from jax.experimental import pallas as pl
from jax.experimental.pallas import tpu as pltpu
from jax.sharding import PartitionSpec as P

WIN = 1024
FREQ = 512
SMOOTH = 64
NW = 8
CORES = 2


def toeplitz_kernel(seed_ref, out_ref):
    rows = 128
    base = jnp.broadcast_to(seed_ref[...], (rows, seed_ref.shape[1]))
    for blk in range(out_ref.shape[0] // rows):
        rolled = pltpu.roll(base, blk * rows, 1, stride=1, stride_axis=0)
        out_ref[blk * rows : (blk + 1) * rows, :] = rolled.astype(out_ref.dtype)


def toeplitz_both(band_taps):
    taps_len = band_taps.shape[0]
    seed = jnp.concatenate(
        [band_taps.astype(jnp.float32), jnp.zeros((taps_len,), jnp.float32)]
    )[None, :]
    return pl.pallas_call(
        toeplitz_kernel,
        out_shape=jax.ShapeDtypeStruct((taps_len, 2 * taps_len), jnp.bfloat16),
    )(seed)


def transform_table(window_len):
    bin_count = window_len // 2
    sample_index = jnp.arange(window_len, dtype=jnp.int32)[:, None]
    bin_index = jnp.arange(bin_count, dtype=jnp.int32)[None, :]
    phase_angle = (sample_index * bin_index % window_len).astype(jnp.float32) * (
        2.0 * math.pi / window_len
    )
    return jnp.concatenate([jnp.cos(phase_angle), -jnp.sin(phase_angle)], axis=1).astype(
        jnp.bfloat16
    )


def band_matrix(bin_count, smooth_len):
    bin_index = jnp.arange(bin_count, dtype=jnp.int32)
    offsets = (bin_index[:, None] - bin_index[None, :]) % bin_count
    half_span = smooth_len // 2
    inside = (offsets < half_span) | (offsets >= bin_count - half_span)
    return inside.astype(jnp.float32)


SUB = 8


def corr_kernel(owner_ref, part_ref, own_ref, *rest, row0):
    out_hbm, scr, sem = rest[-3], rest[-2], rest[-1]
    n_blocks, n_win, rows, freq = part_ref.shape
    n_pairs = owner_ref.shape[0]
    n_top = out_hbm.shape[1]
    row_id = lax.broadcasted_iota(jnp.int32, (rows, freq), 0)
    even = (row_id % 2) == 0
    sign = jnp.where(even, 1.0, -1.0).astype(jnp.float32)

    def one(i, carry):
        slot = i % 2
        s = i // n_top
        k = i % n_top
        b = owner_ref[i]

        @pl.when(i >= 2)
        def _():
            pltpu.make_async_copy(
                scr.at[slot], out_hbm.at[0, 0, pl.ds(row0, rows)], sem.at[slot]
            ).wait()

        acc1 = jnp.zeros((rows // SUB, SUB, freq), jnp.float32)
        acc2 = jnp.zeros((rows // SUB, SUB, freq), jnp.float32)
        for w in range(n_win):
            q = part_ref[b, w].astype(jnp.float32).reshape(rows // SUB, SUB, freq)
            sre = jnp.broadcast_to(own_ref[s, 2 * w : 2 * w + 1, :], (SUB, freq))
            sim = jnp.broadcast_to(own_ref[s, 2 * w + 1 : 2 * w + 2, :], (SUB, freq))
            acc1 = acc1 + q * sre[None]
            acc2 = acc2 + q * sim[None]
        acc1 = acc1.reshape(rows, freq)
        acc2 = acc2.reshape(rows, freq)
        up = pltpu.roll(acc2, rows - 1, 0)
        dn = pltpu.roll(acc2, 1, 0)
        scr[slot] = (sign * acc1 + jnp.where(even, up, dn)).astype(scr.dtype)
        pltpu.make_async_copy(
            scr.at[slot], out_hbm.at[s, k, pl.ds(row0, rows)], sem.at[slot]
        ).start()
        return carry

    lax.fori_loop(0, n_pairs, one, 0)
    for back in range(min(2, n_pairs)):
        last = n_pairs - 1 - back
        pltpu.make_async_copy(
            scr.at[last % 2], out_hbm.at[0, 0, pl.ds(row0, rows)], sem.at[last % 2]
        ).wait()


def correlate(owners, part, own, out_shape, row0, prior=None):
    rows, freq = part.shape[2], part.shape[3]
    in_specs = [
        pl.BlockSpec(memory_space=pltpu.SMEM),
        pl.BlockSpec(memory_space=pltpu.VMEM),
        pl.BlockSpec(memory_space=pltpu.VMEM),
    ]
    args = [owners, part, own]
    aliases = {}
    if prior is not None:
        in_specs.append(pl.BlockSpec(memory_space=pl.ANY))
        args.append(prior)
        aliases = {len(args) - 1: 0}
    return pl.pallas_call(
        functools.partial(corr_kernel, row0=row0),
        out_shape=jax.ShapeDtypeStruct(out_shape, jnp.bfloat16),
        in_specs=in_specs,
        out_specs=pl.BlockSpec(memory_space=pl.ANY),
        scratch_shapes=[
            pltpu.VMEM((2, rows, freq), jnp.bfloat16),
            pltpu.SemaphoreType.DMA((2,)),
        ],
        input_output_aliases=aliases,
        compiler_params=pltpu.CompilerParams(vmem_limit_bytes=40 * 1024 * 1024),
    )(*args)


def shards(records, band_taps, station_owners):
    relayed = lax.all_to_all(records, "tm", split_axis=0, concat_axis=1, tiled=True)
    station_count = relayed.shape[0]
    both_parts = toeplitz_both(band_taps)
    series = relayed.reshape(station_count * NW, WIN)
    halves = jnp.dot(series, both_parts, preferred_element_type=jnp.float32)
    halves = halves.reshape(station_count, NW, 2 * WIN)
    carried = jnp.concatenate(
        [jnp.zeros_like(halves[:, :1, WIN:]), halves[:, :-1, WIN:]], axis=1
    )
    filtered = (halves[:, :, :WIN] + carried).astype(jnp.bfloat16).reshape(-1, WIN)
    spectrum = jnp.dot(filtered, transform_table(WIN), preferred_element_type=jnp.float32)
    real_part = spectrum[:, :FREQ]
    imag_part = spectrum[:, FREQ:]
    power_sum = real_part * real_part + imag_part * imag_part
    smooth = (
        jnp.dot(
            power_sum,
            band_matrix(FREQ, SMOOTH),
            precision=lax.Precision.HIGHEST,
            preferred_element_type=jnp.float32,
        )
        / SMOOTH
    )
    whiten_scale = lax.rsqrt(smooth + 1e-05)
    whitened = (spectrum.reshape(-1, 2, FREQ) * whiten_scale[:, None, :]).astype(jnp.bfloat16)
    whitened = whitened.reshape(station_count, NW, 2, FREQ)
    regrouped = lax.all_to_all(whitened, "tm", split_axis=3, concat_axis=0, tiled=True)
    own_count = regrouped.shape[0]
    freq = regrouped.shape[3]
    contribution = regrouped.transpose(1, 0, 2, 3).reshape(NW, own_count * 2, freq)
    half = own_count
    own = regrouped.astype(jnp.float32).reshape(own_count, NW * 2, freq)
    out_shape = (own_count, station_owners.shape[1], own_count * 2, freq)
    owners = station_owners.reshape(-1)
    first_rows = lax.all_gather(contribution[:, :half], "sta", axis=0, tiled=False)
    second_rows = lax.all_gather(contribution[:, half:], "sta", axis=0, tiled=False)
    result = correlate(owners, first_rows, own, out_shape, 0)
    result = correlate(owners, second_rows, own, out_shape, half, prior=result)
    return result.reshape(own_count, station_owners.shape[1], own_count, 2, freq)


def solution(mesh):
    placed = (P("sta", "tm"), P(), P("sta", None))
    return jax.shard_map(
        shards,
        mesh=mesh,
        in_specs=placed,
        out_specs=P("sta", None, None, None, "tm"),
        check_vma=False,
    )
```

```python
import math

import jax
import jax.numpy as jnp
from jax import lax
from jax.experimental import pallas as pl
from jax.experimental.pallas import tpu as pltpu
from jax.sharding import PartitionSpec as P

WIN = 1024
FREQ = 512
SMOOTH = 64
NW = 8
CORES = 2


def toeplitz_kernel(seed_ref, out_ref):
    rows = 128
    base = jnp.broadcast_to(seed_ref[...], (rows, seed_ref.shape[1]))
    for blk in range(out_ref.shape[0] // rows):
        rolled = pltpu.roll(base, blk * rows, 1, stride=1, stride_axis=0)
        out_ref[blk * rows : (blk + 1) * rows, :] = rolled.astype(out_ref.dtype)


def toeplitz_both(band_taps):
    taps_len = band_taps.shape[0]
    seed = jnp.concatenate(
        [band_taps.astype(jnp.float32), jnp.zeros((taps_len,), jnp.float32)]
    )[None, :]
    return pl.pallas_call(
        toeplitz_kernel,
        out_shape=jax.ShapeDtypeStruct((taps_len, 2 * taps_len), jnp.bfloat16),
    )(seed)


def transform_table(window_len):
    bin_count = window_len // 2
    sample_index = jnp.arange(window_len, dtype=jnp.int32)[:, None]
    bin_index = jnp.arange(bin_count, dtype=jnp.int32)[None, :]
    phase_angle = (sample_index * bin_index % window_len).astype(jnp.float32) * (
        2.0 * math.pi / window_len
    )
    return jnp.concatenate([jnp.cos(phase_angle), -jnp.sin(phase_angle)], axis=1).astype(
        jnp.bfloat16
    )


def band_matrix(bin_count, smooth_len):
    bin_index = jnp.arange(bin_count, dtype=jnp.int32)
    offsets = (bin_index[:, None] - bin_index[None, :]) % bin_count
    half_span = smooth_len // 2
    inside = (offsets < half_span) | (offsets >= bin_count - half_span)
    return inside.astype(jnp.float32)


PACK = 16


def corr_kernel(owner_ref, part_ref, own_ref, out_hbm, scr, sem):
    rows, freq = part_ref.shape[2], part_ref.shape[3]
    n_win = part_ref.shape[1]
    n_pairs = owner_ref.shape[0]
    n_top = out_hbm.shape[1]
    row_id = lax.broadcasted_iota(jnp.int32, (rows, freq), 0)
    even = (row_id % 2) == 0
    sign = jnp.where(even, 1.0, -1.0).astype(jnp.float32)

    def one(i, carry):
        slot = i % 2
        s = i // n_top
        k = i % n_top
        b = owner_ref[i]

        @pl.when(i >= 2)
        def _():
            pltpu.make_async_copy(scr.at[slot], out_hbm.at[0, 0], sem.at[slot]).wait()

        acc1 = jnp.zeros((rows // PACK, PACK, freq), jnp.bfloat16)
        acc2 = jnp.zeros((rows // PACK, PACK, freq), jnp.bfloat16)
        for w in range(n_win):
            q = part_ref[b, w].reshape(rows // PACK, PACK, freq)
            sre = jnp.broadcast_to(own_ref[s, 2 * w : 2 * w + 1, :], (PACK, freq))
            sim = jnp.broadcast_to(own_ref[s, 2 * w + 1 : 2 * w + 2, :], (PACK, freq))
            acc1 = acc1 + q * sre.astype(jnp.bfloat16)[None]
            acc2 = acc2 + q * sim.astype(jnp.bfloat16)[None]
        acc1 = acc1.reshape(rows, freq).astype(jnp.float32)
        acc2 = acc2.reshape(rows, freq).astype(jnp.float32)
        up = pltpu.roll(acc2, rows - 1, 0)
        dn = pltpu.roll(acc2, 1, 0)
        scr[slot] = (sign * acc1 + jnp.where(even, up, dn)).astype(scr.dtype)
        pltpu.make_async_copy(scr.at[slot], out_hbm.at[s, k], sem.at[slot]).start()
        return carry

    lax.fori_loop(0, n_pairs, one, 0)
    for back in range(min(2, n_pairs)):
        last = n_pairs - 1 - back
        pltpu.make_async_copy(scr.at[last % 2], out_hbm.at[0, 0], sem.at[last % 2]).wait()


def correlate(owners, part, own, out_shape):
    rows, freq = part.shape[2], part.shape[3]
    return pl.pallas_call(
        corr_kernel,
        out_shape=jax.ShapeDtypeStruct(out_shape, jnp.bfloat16),
        in_specs=[
            pl.BlockSpec(memory_space=pltpu.SMEM),
            pl.BlockSpec(memory_space=pltpu.VMEM),
            pl.BlockSpec(memory_space=pltpu.VMEM),
        ],
        out_specs=pl.BlockSpec(memory_space=pl.ANY),
        scratch_shapes=[pltpu.VMEM((2, rows, freq), jnp.bfloat16), pltpu.SemaphoreType.DMA((2,))],
        compiler_params=pltpu.CompilerParams(vmem_limit_bytes=48 * 1024 * 1024),
    )(owners, part, own)


def shards(records, band_taps, station_owners):
    relayed = lax.all_to_all(records, "tm", split_axis=0, concat_axis=1, tiled=True)
    station_count = relayed.shape[0]
    both_parts = toeplitz_both(band_taps)
    series = relayed.reshape(station_count * NW, WIN)
    halves = jnp.dot(series, both_parts, preferred_element_type=jnp.float32)
    halves = halves.reshape(station_count, NW, 2 * WIN)
    carried = jnp.concatenate(
        [jnp.zeros_like(halves[:, :1, WIN:]), halves[:, :-1, WIN:]], axis=1
    )
    filtered = (halves[:, :, :WIN] + carried).astype(jnp.bfloat16).reshape(-1, WIN)
    spectrum = jnp.dot(filtered, transform_table(WIN), preferred_element_type=jnp.float32)
    real_part = spectrum[:, :FREQ]
    imag_part = spectrum[:, FREQ:]
    power_sum = real_part * real_part + imag_part * imag_part
    smooth = (
        jnp.dot(
            power_sum,
            band_matrix(FREQ, SMOOTH),
            precision=lax.Precision.HIGHEST,
            preferred_element_type=jnp.float32,
        )
        / SMOOTH
    )
    whiten_scale = lax.rsqrt(smooth + 1e-05)
    whitened = (spectrum.reshape(-1, 2, FREQ) * whiten_scale[:, None, :]).astype(jnp.bfloat16)
    whitened = whitened.reshape(station_count, NW, 2, FREQ)
    regrouped = lax.all_to_all(whitened, "tm", split_axis=3, concat_axis=0, tiled=True)
    own_count = regrouped.shape[0]
    freq = regrouped.shape[3]
    contribution = regrouped.transpose(1, 0, 2, 3).reshape(NW, own_count * 2, freq)
    gathered = lax.all_gather(contribution, "sta", axis=0, tiled=False)
    own = regrouped.astype(jnp.float32).reshape(own_count, NW * 2, freq)
    out_shape = (own_count, station_owners.shape[1], own_count * 2, freq)
    result = correlate(station_owners.reshape(-1), gathered, own, out_shape)
    return result.reshape(own_count, station_owners.shape[1], own_count, 2, freq)


def solution(mesh):
    placed = (P("sta", "tm"), P(), P("sta", None))
    return jax.shard_map(
        shards,
        mesh=mesh,
        in_specs=placed,
        out_specs=P("sta", None, None, None, "tm"),
        check_vma=False,
    )
```

```python
import math

import jax
import jax.numpy as jnp
from jax import lax
from jax.experimental import pallas as pl
from jax.experimental.pallas import tpu as pltpu
from jax.sharding import PartitionSpec as P

WIN = 1024
FREQ = 512
SMOOTH = 64
NW = 8
CORES = 2


def toeplitz_kernel(seed_ref, out_ref):
    rows = 128
    base = jnp.broadcast_to(seed_ref[...], (rows, seed_ref.shape[1]))
    for blk in range(out_ref.shape[0] // rows):
        rolled = pltpu.roll(base, blk * rows, 1, stride=1, stride_axis=0)
        out_ref[blk * rows : (blk + 1) * rows, :] = rolled.astype(out_ref.dtype)


def toeplitz_both(band_taps):
    taps_len = band_taps.shape[0]
    seed = jnp.concatenate(
        [band_taps.astype(jnp.float32), jnp.zeros((taps_len,), jnp.float32)]
    )[None, :]
    return pl.pallas_call(
        toeplitz_kernel,
        out_shape=jax.ShapeDtypeStruct((taps_len, 2 * taps_len), jnp.bfloat16),
    )(seed)


def transform_table(window_len):
    bin_count = window_len // 2
    sample_index = jnp.arange(window_len, dtype=jnp.int32)[:, None]
    bin_index = jnp.arange(bin_count, dtype=jnp.int32)[None, :]
    phase_angle = (sample_index * bin_index % window_len).astype(jnp.float32) * (
        2.0 * math.pi / window_len
    )
    return jnp.concatenate([jnp.cos(phase_angle), -jnp.sin(phase_angle)], axis=1).astype(
        jnp.bfloat16
    )


def band_matrix(bin_count, smooth_len):
    bin_index = jnp.arange(bin_count, dtype=jnp.int32)
    offsets = (bin_index[:, None] - bin_index[None, :]) % bin_count
    half_span = smooth_len // 2
    inside = (offsets < half_span) | (offsets >= bin_count - half_span)
    return inside.astype(jnp.float32)


ROWS = 32


def corr_kernel(owner_ref, part_hbm, own_ref, out_hbm, buf, scr, in_sem, out_sem):
    rows_all, freq = buf.shape[2], buf.shape[3]
    n_pairs = owner_ref.shape[0]
    n_top = out_hbm.shape[1]
    chunk = min(ROWS, rows_all)
    row_id = lax.broadcasted_iota(jnp.int32, (chunk, freq), 0)
    even = (row_id % 2) == 0
    sign = jnp.where(even, 1.0, -1.0).astype(jnp.float32)

    def fetch(i, slot):
        return pltpu.make_async_copy(part_hbm.at[owner_ref[i]], buf.at[slot], in_sem.at[slot])

    fetch(0, 0).start()

    def one(i, carry):
        slot = i % 2
        s = i // n_top
        k = i % n_top
        fetch(i, slot).wait()

        @pl.when(i + 1 < n_pairs)
        def _():
            fetch(i + 1, 1 - slot).start()

        @pl.when(i >= 2)
        def _():
            pltpu.make_async_copy(scr.at[slot], out_hbm.at[0, 0], out_sem.at[slot]).wait()

        for c0 in range(0, rows_all, chunk):
            acc1 = jnp.zeros((chunk, freq), jnp.float32)
            acc2 = jnp.zeros((chunk, freq), jnp.float32)
            for w in range(buf.shape[1]):
                q = buf[slot, w, c0 : c0 + chunk, :].astype(jnp.float32)
                sre = own_ref[s, 2 * w : 2 * w + 1, :]
                sim = own_ref[s, 2 * w + 1 : 2 * w + 2, :]
                acc1 = acc1 + q * sre
                acc2 = acc2 + q * sim
            up = pltpu.roll(acc2, chunk - 1, 0)
            dn = pltpu.roll(acc2, 1, 0)
            res = sign * acc1 + jnp.where(even, up, dn)
            scr[slot, c0 : c0 + chunk, :] = res.astype(scr.dtype)
        pltpu.make_async_copy(scr.at[slot], out_hbm.at[s, k], out_sem.at[slot]).start()
        return carry

    lax.fori_loop(0, n_pairs, one, 0)
    for back in range(min(2, n_pairs)):
        last = n_pairs - 1 - back
        pltpu.make_async_copy(scr.at[last % 2], out_hbm.at[0, 0], out_sem.at[last % 2]).wait()


def correlate(owners, part, own, out_shape):
    n_win, rows, freq = part.shape[1], part.shape[2], part.shape[3]
    return pl.pallas_call(
        corr_kernel,
        out_shape=jax.ShapeDtypeStruct(out_shape, jnp.bfloat16),
        in_specs=[
            pl.BlockSpec(memory_space=pltpu.SMEM),
            pl.BlockSpec(memory_space=pl.ANY),
            pl.BlockSpec(memory_space=pltpu.VMEM),
        ],
        out_specs=pl.BlockSpec(memory_space=pl.ANY),
        scratch_shapes=[
            pltpu.VMEM((2, n_win, rows, freq), jnp.bfloat16),
            pltpu.VMEM((2, rows, freq), jnp.bfloat16),
            pltpu.SemaphoreType.DMA((2,)),
            pltpu.SemaphoreType.DMA((2,)),
        ],
    )(owners, part, own)


def shards(records, band_taps, station_owners):
    relayed = lax.all_to_all(records, "tm", split_axis=0, concat_axis=1, tiled=True)
    station_count = relayed.shape[0]
    both_parts = toeplitz_both(band_taps)
    series = relayed.reshape(station_count * NW, WIN)
    halves = jnp.dot(series, both_parts, preferred_element_type=jnp.float32)
    halves = halves.reshape(station_count, NW, 2 * WIN)
    carried = jnp.concatenate(
        [jnp.zeros_like(halves[:, :1, WIN:]), halves[:, :-1, WIN:]], axis=1
    )
    filtered = (halves[:, :, :WIN] + carried).astype(jnp.bfloat16).reshape(-1, WIN)
    spectrum = jnp.dot(filtered, transform_table(WIN), preferred_element_type=jnp.float32)
    real_part = spectrum[:, :FREQ]
    imag_part = spectrum[:, FREQ:]
    power_sum = real_part * real_part + imag_part * imag_part
    smooth = (
        jnp.dot(
            power_sum,
            band_matrix(FREQ, SMOOTH),
            precision=lax.Precision.HIGHEST,
            preferred_element_type=jnp.float32,
        )
        / SMOOTH
    )
    whiten_scale = lax.rsqrt(smooth + 1e-05)
    whitened = (spectrum.reshape(-1, 2, FREQ) * whiten_scale[:, None, :]).astype(jnp.bfloat16)
    whitened = whitened.reshape(station_count, NW, 2, FREQ)
    regrouped = lax.all_to_all(whitened, "tm", split_axis=3, concat_axis=0, tiled=True)
    own_count = regrouped.shape[0]
    freq = regrouped.shape[3]
    contribution = regrouped.transpose(1, 0, 2, 3).reshape(NW, own_count * 2, freq)
    gathered = lax.all_gather(contribution, "sta", axis=0, tiled=False)
    own = regrouped.astype(jnp.float32).reshape(own_count, NW * 2, freq)
    out_shape = (own_count, station_owners.shape[1], own_count * 2, freq)
    result = correlate(station_owners.reshape(-1), gathered, own, out_shape)
    return result.reshape(own_count, station_owners.shape[1], own_count, 2, freq)


def solution(mesh):
    placed = (P("sta", "tm"), P(), P("sta", None))
    return jax.shard_map(
        shards,
        mesh=mesh,
        in_specs=placed,
        out_specs=P("sta", None, None, None, "tm"),
        check_vma=False,
    )
```

```python
import math

import jax
import jax.numpy as jnp
from jax import lax
from jax.experimental import pallas as pl
from jax.experimental.pallas import tpu as pltpu
from jax.sharding import PartitionSpec as P

WIN = 1024
FREQ = 512
SMOOTH = 64
NW = 8
CORES = 2


def toeplitz_kernel(seed_ref, out_ref):
    rows = 128
    base = jnp.broadcast_to(seed_ref[...], (rows, seed_ref.shape[1]))
    for blk in range(out_ref.shape[0] // rows):
        rolled = pltpu.roll(base, blk * rows, 1, stride=1, stride_axis=0)
        out_ref[blk * rows : (blk + 1) * rows, :] = rolled.astype(out_ref.dtype)


def toeplitz_both(band_taps):
    taps_len = band_taps.shape[0]
    seed = jnp.concatenate(
        [band_taps.astype(jnp.float32), jnp.zeros((taps_len,), jnp.float32)]
    )[None, :]
    return pl.pallas_call(
        toeplitz_kernel,
        out_shape=jax.ShapeDtypeStruct((taps_len, 2 * taps_len), jnp.bfloat16),
    )(seed)


def transform_table(window_len, quarters):
    bin_count = window_len // 2
    per_quarter = bin_count // quarters
    sample_index = jnp.arange(window_len, dtype=jnp.int32)[:, None, None]
    bin_index = (
        jnp.arange(quarters, dtype=jnp.int32)[None, :, None] * per_quarter
        + jnp.arange(per_quarter, dtype=jnp.int32)[None, None, :]
    )
    phase_angle = (sample_index * bin_index % window_len).astype(jnp.float32) * (
        2.0 * math.pi / window_len
    )
    table = jnp.stack([jnp.cos(phase_angle), -jnp.sin(phase_angle)], axis=2)
    return table.reshape(window_len, 2 * bin_count).astype(jnp.bfloat16)


def band_matrix(bin_count, smooth_len):
    bin_index = jnp.arange(bin_count, dtype=jnp.int32)
    offsets = (bin_index[:, None] - bin_index[None, :]) % bin_count
    half_span = smooth_len // 2
    inside = (offsets < half_span) | (offsets >= bin_count - half_span)
    return inside.astype(jnp.float32)


ROWS = 32


def corr_kernel(owner_ref, part_ref, own_ref, out_hbm, scr, sem):
    rows_all, freq = part_ref.shape[2], part_ref.shape[3]
    n_pairs = owner_ref.shape[0]
    n_top = out_hbm.shape[1]
    chunk = min(ROWS, rows_all)
    row_id = lax.broadcasted_iota(jnp.int32, (chunk, freq), 0)
    even = (row_id % 2) == 0
    sign = jnp.where(even, 1.0, -1.0).astype(jnp.float32)

    def one(i, carry):
        slot = i % 2
        s = i // n_top
        k = i % n_top
        b = owner_ref[i]

        @pl.when(i >= 2)
        def _():
            pltpu.make_async_copy(scr.at[slot], out_hbm.at[0, 0], sem.at[slot]).wait()

        for c0 in range(0, rows_all, chunk):
            acc1 = jnp.zeros((chunk, freq), jnp.float32)
            acc2 = jnp.zeros((chunk, freq), jnp.float32)
            for w in range(NW):
                q = part_ref[b, w, c0 : c0 + chunk, :].astype(jnp.float32)
                sre = own_ref[w, pl.ds(2 * s, 1), :]
                sim = own_ref[w, pl.ds(2 * s + 1, 1), :]
                acc1 = acc1 + q * sre
                acc2 = acc2 + q * sim
            up = pltpu.roll(acc2, chunk - 1, 0)
            dn = pltpu.roll(acc2, 1, 0)
            res = sign * acc1 + jnp.where(even, up, dn)
            scr[slot, c0 : c0 + chunk, :] = res.astype(scr.dtype)
        pltpu.make_async_copy(scr.at[slot], out_hbm.at[s, k], sem.at[slot]).start()
        return carry

    lax.fori_loop(0, n_pairs, one, 0)
    for back in range(min(2, n_pairs)):
        last = n_pairs - 1 - back
        pltpu.make_async_copy(scr.at[last % 2], out_hbm.at[0, 0], sem.at[last % 2]).wait()


def correlate(owners, part, own, out_shape):
    rows, freq = part.shape[2], part.shape[3]
    return pl.pallas_call(
        corr_kernel,
        out_shape=jax.ShapeDtypeStruct(out_shape, jnp.bfloat16),
        in_specs=[
            pl.BlockSpec(memory_space=pltpu.SMEM),
            pl.BlockSpec(memory_space=pltpu.VMEM),
            pl.BlockSpec(memory_space=pltpu.VMEM),
        ],
        out_specs=pl.BlockSpec(memory_space=pl.ANY),
        scratch_shapes=[pltpu.VMEM((2, rows, freq), jnp.bfloat16), pltpu.SemaphoreType.DMA((2,))],
        compiler_params=pltpu.CompilerParams(vmem_limit_bytes=48 * 1024 * 1024),
    )(owners, part, own)


def shards(records, band_taps, station_owners):
    relayed = lax.all_to_all(records, "tm", split_axis=0, concat_axis=1, tiled=True)
    station_count = relayed.shape[0]
    both_parts = toeplitz_both(band_taps)
    series = relayed.reshape(station_count * NW, WIN)
    halves = jnp.dot(series, both_parts, preferred_element_type=jnp.float32)
    halves = halves.reshape(station_count, NW, 2 * WIN)
    carried = jnp.concatenate(
        [jnp.zeros_like(halves[:, :1, WIN:]), halves[:, :-1, WIN:]], axis=1
    )
    filtered = (halves[:, :, :WIN] + carried).astype(jnp.bfloat16).reshape(-1, WIN)
    quarters = records.shape[0] // station_count
    per_quarter = FREQ // quarters
    spectrum = jnp.dot(
        filtered, transform_table(WIN, quarters), preferred_element_type=jnp.float32
    ).reshape(-1, quarters, 2, per_quarter)
    power_sum = (
        spectrum[:, :, 0] * spectrum[:, :, 0] + spectrum[:, :, 1] * spectrum[:, :, 1]
    ).reshape(-1, FREQ)
    smooth = (
        jnp.dot(
            power_sum,
            band_matrix(FREQ, SMOOTH),
            precision=lax.Precision.HIGHEST,
            preferred_element_type=jnp.float32,
        )
        / SMOOTH
    )
    whiten_scale = lax.rsqrt(smooth + 1e-05).reshape(-1, quarters, 1, per_quarter)
    whitened = (spectrum * whiten_scale).astype(jnp.bfloat16)
    whitened = whitened.reshape(station_count, NW, quarters, 2, per_quarter).transpose(
        2, 1, 0, 3, 4
    )
    contribution = lax.all_to_all(whitened, "tm", split_axis=0, concat_axis=2, tiled=True)
    own_count = contribution.shape[2]
    contribution = contribution.reshape(NW, own_count * 2, per_quarter)
    gathered = lax.all_gather(contribution, "sta", axis=0, tiled=False)
    own = contribution.astype(jnp.float32)
    out_shape = (own_count, station_owners.shape[1], own_count * 2, per_quarter)
    result = correlate(station_owners.reshape(-1), gathered, own, out_shape)
    return result.reshape(own_count, station_owners.shape[1], own_count, 2, per_quarter)


def solution(mesh):
    placed = (P("sta", "tm"), P(), P("sta", None))
    return jax.shard_map(
        shards,
        mesh=mesh,
        in_specs=placed,
        out_specs=P("sta", None, None, None, "tm"),
        check_vma=False,
    )
```

```python
import math

import jax
import numpy as np
import jax.numpy as jnp
from jax import lax
from jax.experimental import pallas as pl
from jax.experimental.pallas import tpu as pltpu
from jax.sharding import PartitionSpec as P

WIN = 1024
FREQ = 512
SMOOTH = 64
NW = 8
CORES = 2


def toeplitz_kernel(seed_ref, out_ref):
    rows = 128
    base = jnp.broadcast_to(seed_ref[...], (rows, seed_ref.shape[1]))
    for blk in range(out_ref.shape[0] // rows):
        rolled = pltpu.roll(base, blk * rows, 1, stride=1, stride_axis=0)
        out_ref[blk * rows : (blk + 1) * rows, :] = rolled.astype(out_ref.dtype)


def toeplitz_both(band_taps):
    taps_len = band_taps.shape[0]
    seed = jnp.concatenate(
        [band_taps.astype(jnp.float32), jnp.zeros((taps_len,), jnp.float32)]
    )[None, :]
    return pl.pallas_call(
        toeplitz_kernel,
        out_shape=jax.ShapeDtypeStruct((taps_len, 2 * taps_len), jnp.bfloat16),
    )(seed)


def transform_table(window_len, quarters):
    bin_count = window_len // 2
    per_quarter = bin_count // quarters
    sample_index = np.arange(window_len, dtype=np.int64)[:, None, None]
    bin_index = (
        np.arange(quarters, dtype=np.int64)[None, :, None] * per_quarter
        + np.arange(per_quarter, dtype=np.int64)[None, None, :]
    )
    phase_angle = (sample_index * bin_index % window_len).astype(np.float32) * np.float32(
        2.0 * math.pi / window_len
    )
    table = np.stack([np.cos(phase_angle), -np.sin(phase_angle)], axis=2)
    return jnp.asarray(table.reshape(window_len, 2 * bin_count).astype(jnp.bfloat16))


def band_matrix(bin_count, smooth_len):
    bin_index = jnp.arange(bin_count, dtype=jnp.int32)
    offsets = (bin_index[:, None] - bin_index[None, :]) % bin_count
    half_span = smooth_len // 2
    inside = (offsets < half_span) | (offsets >= bin_count - half_span)
    return inside.astype(jnp.float32)


ROWS = 32


def corr_kernel(owner_ref, part_ref, own_ref, out_hbm, scr, sem):
    rows_all, freq = part_ref.shape[2], part_ref.shape[3]
    n_pairs = owner_ref.shape[0]
    n_top = out_hbm.shape[1]
    chunk = min(ROWS, rows_all)
    row_id = lax.broadcasted_iota(jnp.int32, (chunk, freq), 0)
    even = (row_id % 2) == 0
    sign = jnp.where(even, 1.0, -1.0).astype(jnp.float32)

    def one(i, carry):
        slot = i % 2
        s = i // n_top
        k = i % n_top
        b = owner_ref[i]

        @pl.when(i >= 2)
        def _():
            pltpu.make_async_copy(scr.at[slot], out_hbm.at[0, 0], sem.at[slot]).wait()

        for c0 in range(0, rows_all, chunk):
            acc1 = jnp.zeros((chunk, freq), jnp.float32)
            acc2 = jnp.zeros((chunk, freq), jnp.float32)
            for w in range(NW):
                q = part_ref[b, w, c0 : c0 + chunk, :].astype(jnp.float32)
                sre = own_ref[w, pl.ds(2 * s, 1), :]
                sim = own_ref[w, pl.ds(2 * s + 1, 1), :]
                acc1 = acc1 + q * sre
                acc2 = acc2 + q * sim
            up = pltpu.roll(acc2, chunk - 1, 0)
            dn = pltpu.roll(acc2, 1, 0)
            res = sign * acc1 + jnp.where(even, up, dn)
            scr[slot, c0 : c0 + chunk, :] = res.astype(scr.dtype)
        pltpu.make_async_copy(scr.at[slot], out_hbm.at[s, k], sem.at[slot]).start()
        return carry

    lax.fori_loop(0, n_pairs, one, 0)
    for back in range(min(2, n_pairs)):
        last = n_pairs - 1 - back
        pltpu.make_async_copy(scr.at[last % 2], out_hbm.at[0, 0], sem.at[last % 2]).wait()


def correlate(owners, part, own, out_shape):
    rows, freq = part.shape[2], part.shape[3]
    return pl.pallas_call(
        corr_kernel,
        out_shape=jax.ShapeDtypeStruct(out_shape, jnp.bfloat16),
        in_specs=[
            pl.BlockSpec(memory_space=pltpu.SMEM),
            pl.BlockSpec(memory_space=pltpu.VMEM),
            pl.BlockSpec(memory_space=pltpu.VMEM),
        ],
        out_specs=pl.BlockSpec(memory_space=pl.ANY),
        scratch_shapes=[pltpu.VMEM((2, rows, freq), jnp.bfloat16), pltpu.SemaphoreType.DMA((2,))],
        compiler_params=pltpu.CompilerParams(vmem_limit_bytes=48 * 1024 * 1024),
    )(owners, part, own)


def shards(records, band_taps, station_owners):
    relayed = lax.all_to_all(records, "tm", split_axis=0, concat_axis=1, tiled=True)
    station_count = relayed.shape[0]
    both_parts = toeplitz_both(band_taps)
    series = relayed.reshape(station_count * NW, WIN)
    halves = jnp.dot(series, both_parts, preferred_element_type=jnp.float32)
    halves = halves.reshape(station_count, NW, 2 * WIN)
    carried = jnp.concatenate(
        [jnp.zeros_like(halves[:, :1, WIN:]), halves[:, :-1, WIN:]], axis=1
    )
    filtered = (halves[:, :, :WIN] + carried).astype(jnp.bfloat16).reshape(-1, WIN)
    quarters = records.shape[0] // station_count
    per_quarter = FREQ // quarters
    spectrum = jnp.dot(
        filtered, transform_table(WIN, quarters), preferred_element_type=jnp.float32
    ).reshape(-1, quarters, 2, per_quarter)
    power_sum = (
        spectrum[:, :, 0] * spectrum[:, :, 0] + spectrum[:, :, 1] * spectrum[:, :, 1]
    ).reshape(-1, FREQ)
    smooth = (
        jnp.dot(
            power_sum,
            band_matrix(FREQ, SMOOTH),
            precision=lax.Precision.HIGHEST,
            preferred_element_type=jnp.float32,
        )
        / SMOOTH
    )
    whiten_scale = lax.rsqrt(smooth + 1e-05).reshape(-1, quarters, 1, per_quarter)
    whitened = (spectrum * whiten_scale).astype(jnp.bfloat16)
    whitened = whitened.reshape(station_count, NW, quarters, 2, per_quarter).transpose(
        2, 1, 0, 3, 4
    )
    contribution = lax.all_to_all(whitened, "tm", split_axis=0, concat_axis=2, tiled=True)
    own_count = contribution.shape[2]
    contribution = contribution.reshape(NW, own_count * 2, per_quarter)
    gathered = lax.all_gather(contribution, "sta", axis=0, tiled=False)
    own = contribution.astype(jnp.float32)
    out_shape = (own_count, station_owners.shape[1], own_count * 2, per_quarter)
    result = correlate(station_owners.reshape(-1), gathered, own, out_shape)
    return result.reshape(own_count, station_owners.shape[1], own_count, 2, per_quarter)


def solution(mesh):
    placed = (P("sta", "tm"), P(), P("sta", None))
    return jax.shard_map(
        shards,
        mesh=mesh,
        in_specs=placed,
        out_specs=P("sta", None, None, None, "tm"),
        check_vma=False,
    )
```

```python
import math

import jax
import numpy as np
import jax.numpy as jnp
from jax import lax
from jax.experimental import pallas as pl
from jax.experimental.pallas import tpu as pltpu
from jax.sharding import PartitionSpec as P

WIN = 1024
FREQ = 512
SMOOTH = 64
NW = 8
CORES = 2


def toeplitz_kernel(seed_ref, out_ref):
    rows = 128
    base = jnp.broadcast_to(seed_ref[...], (rows, seed_ref.shape[1]))
    for blk in range(out_ref.shape[0] // rows):
        rolled = pltpu.roll(base, blk * rows, 1, stride=1, stride_axis=0)
        out_ref[blk * rows : (blk + 1) * rows, :] = rolled.astype(out_ref.dtype)


def toeplitz_both(band_taps):
    taps_len = band_taps.shape[0]
    seed = jnp.concatenate(
        [band_taps.astype(jnp.float32), jnp.zeros((taps_len,), jnp.float32)]
    )[None, :]
    return pl.pallas_call(
        toeplitz_kernel,
        out_shape=jax.ShapeDtypeStruct((taps_len, 2 * taps_len), jnp.bfloat16),
    )(seed)


def transform_table(window_len, quarters):
    bin_count = window_len // 2
    per_quarter = bin_count // quarters
    sample_index = np.arange(window_len, dtype=np.int64)[:, None, None]
    bin_index = (
        np.arange(quarters, dtype=np.int64)[None, :, None] * per_quarter
        + np.arange(per_quarter, dtype=np.int64)[None, None, :]
    )
    phase_angle = (sample_index * bin_index % window_len).astype(np.float32) * np.float32(
        2.0 * math.pi / window_len
    )
    table = np.stack([np.cos(phase_angle), -np.sin(phase_angle)], axis=2)
    return jnp.asarray(table.reshape(window_len, 2 * bin_count).astype(jnp.bfloat16))


def band_matrix(bin_count, smooth_len):
    bin_index = jnp.arange(bin_count, dtype=jnp.int32)
    offsets = (bin_index[:, None] - bin_index[None, :]) % bin_count
    half_span = smooth_len // 2
    inside = (offsets < half_span) | (offsets >= bin_count - half_span)
    return inside.astype(jnp.float32)


ROWS = 32


def corr_kernel(order_ref, blk_ref, bound_ref, part_ref, own_ref, out_hbm, scr, sem):
    h = pl.program_id(0)
    n_half, n_win, rows_all, freq = part_ref.shape
    n_pairs = order_ref.shape[0]
    n_top = out_hbm.shape[1]
    chunk = min(ROWS, rows_all)
    row_id = lax.broadcasted_iota(jnp.int32, (chunk, freq), 0)
    even = (row_id % 2) == 0
    sign = jnp.where(even, 1.0, -1.0).astype(jnp.float32)

    def one(i, carry):
        slot = i % 2
        p = order_ref[i]
        s = p // n_top
        k = p % n_top
        b = blk_ref[i] - h * n_half

        @pl.when(i >= 2)
        def _():
            pltpu.make_async_copy(scr.at[slot], out_hbm.at[0, 0], sem.at[slot]).wait()

        for c0 in range(0, rows_all, chunk):
            acc1 = jnp.zeros((chunk, freq), jnp.float32)
            acc2 = jnp.zeros((chunk, freq), jnp.float32)
            for w in range(n_win):
                q = part_ref[b, w, c0 : c0 + chunk, :].astype(jnp.float32)
                sre = own_ref[w, pl.ds(2 * s, 1), :]
                sim = own_ref[w, pl.ds(2 * s + 1, 1), :]
                acc1 = acc1 + q * sre
                acc2 = acc2 + q * sim
            up = pltpu.roll(acc2, chunk - 1, 0)
            dn = pltpu.roll(acc2, 1, 0)
            res = sign * acc1 + jnp.where(even, up, dn)
            scr[slot, c0 : c0 + chunk, :] = res.astype(scr.dtype)
        pltpu.make_async_copy(scr.at[slot], out_hbm.at[s, k], sem.at[slot]).start()
        return carry

    lax.fori_loop(bound_ref[h], bound_ref[h + 1], one, 0)

    @pl.when(h == pl.num_programs(0) - 1)
    def _():
        for back in range(min(2, n_pairs)):
            last = n_pairs - 1 - back
            pltpu.make_async_copy(scr.at[last % 2], out_hbm.at[0, 0], sem.at[last % 2]).wait()


def correlate(owners, part, own, out_shape):
    n_blocks, n_win, rows, freq = part.shape
    n_half = n_blocks // 2
    late = (owners >= n_half).astype(jnp.int32)
    order = jnp.argsort(late, stable=True).astype(jnp.int32)
    blk = owners[order].astype(jnp.int32)
    n_early = owners.shape[0] - jnp.sum(late)
    bounds = jnp.stack([jnp.zeros((), jnp.int32), n_early.astype(jnp.int32), jnp.full((), owners.shape[0], jnp.int32)])
    grid_spec = pltpu.PrefetchScalarGridSpec(
        num_scalar_prefetch=3,
        grid=(2,),
        in_specs=[
            pl.BlockSpec((n_half, n_win, rows, freq), lambda h, *_: (h, 0, 0, 0)),
            pl.BlockSpec(own.shape, lambda h, *_: (0, 0, 0)),
        ],
        out_specs=pl.BlockSpec(memory_space=pl.ANY),
        scratch_shapes=[
            pltpu.VMEM((2, rows, freq), jnp.bfloat16),
            pltpu.SemaphoreType.DMA((2,)),
        ],
    )
    return pl.pallas_call(
        corr_kernel,
        out_shape=jax.ShapeDtypeStruct(out_shape, jnp.bfloat16),
        grid_spec=grid_spec,
        compiler_params=pltpu.CompilerParams(
            dimension_semantics=("arbitrary",), vmem_limit_bytes=48 * 1024 * 1024
        ),
    )(order, blk, bounds, part, own)


def shards(records, band_taps, station_owners):
    relayed = lax.all_to_all(records, "tm", split_axis=0, concat_axis=1, tiled=True)
    station_count = relayed.shape[0]
    both_parts = toeplitz_both(band_taps)
    series = relayed.reshape(station_count * NW, WIN)
    halves = jnp.dot(series, both_parts, preferred_element_type=jnp.float32)
    halves = halves.reshape(station_count, NW, 2 * WIN)
    carried = jnp.concatenate(
        [jnp.zeros_like(halves[:, :1, WIN:]), halves[:, :-1, WIN:]], axis=1
    )
    filtered = (halves[:, :, :WIN] + carried).astype(jnp.bfloat16).reshape(-1, WIN)
    quarters = records.shape[0] // station_count
    per_quarter = FREQ // quarters
    spectrum = jnp.dot(
        filtered, transform_table(WIN, quarters), preferred_element_type=jnp.float32
    ).reshape(-1, quarters, 2, per_quarter)
    power_sum = (
        spectrum[:, :, 0] * spectrum[:, :, 0] + spectrum[:, :, 1] * spectrum[:, :, 1]
    ).reshape(-1, FREQ)
    smooth = (
        jnp.dot(
            power_sum,
            band_matrix(FREQ, SMOOTH),
            precision=lax.Precision.HIGHEST,
            preferred_element_type=jnp.float32,
        )
        / SMOOTH
    )
    whiten_scale = lax.rsqrt(smooth + 1e-05).reshape(-1, quarters, 1, per_quarter)
    whitened = (spectrum * whiten_scale).astype(jnp.bfloat16)
    whitened = whitened.reshape(station_count, NW, quarters, 2, per_quarter).transpose(
        2, 1, 0, 3, 4
    )
    contribution = lax.all_to_all(whitened, "tm", split_axis=0, concat_axis=2, tiled=True)
    own_count = contribution.shape[2]
    contribution = contribution.reshape(NW, own_count * 2, per_quarter)
    gathered = lax.all_gather(contribution, "sta", axis=0, tiled=False)
    own = contribution.astype(jnp.float32)
    out_shape = (own_count, station_owners.shape[1], own_count * 2, per_quarter)
    result = correlate(station_owners.reshape(-1), gathered, own, out_shape)
    return result.reshape(own_count, station_owners.shape[1], own_count, 2, per_quarter)


def solution(mesh):
    placed = (P("sta", "tm"), P(), P("sta", None))
    return jax.shard_map(
        shards,
        mesh=mesh,
        in_specs=placed,
        out_specs=P("sta", None, None, None, "tm"),
        check_vma=False,
    )
```

```python
import math

import jax
import numpy as np
import jax.numpy as jnp
from jax import lax
from jax.experimental import pallas as pl
from jax.experimental.pallas import tpu as pltpu
from jax.sharding import PartitionSpec as P

WIN = 1024
FREQ = 512
SMOOTH = 64
NW = 8
CORES = 2


def toeplitz_kernel(seed_ref, out_ref):
    rows = 128
    base = jnp.broadcast_to(seed_ref[...], (rows, seed_ref.shape[1]))
    for blk in range(out_ref.shape[0] // rows):
        rolled = pltpu.roll(base, blk * rows, 1, stride=1, stride_axis=0)
        out_ref[blk * rows : (blk + 1) * rows, :] = rolled.astype(out_ref.dtype)


def toeplitz_both(band_taps):
    taps_len = band_taps.shape[0]
    seed = jnp.concatenate(
        [band_taps.astype(jnp.float32), jnp.zeros((taps_len,), jnp.float32)]
    )[None, :]
    return pl.pallas_call(
        toeplitz_kernel,
        out_shape=jax.ShapeDtypeStruct((taps_len, 2 * taps_len), jnp.bfloat16),
    )(seed)


def transform_table(window_len, quarters):
    bin_count = window_len // 2
    per_quarter = bin_count // quarters
    sample_index = np.arange(window_len, dtype=np.int64)[:, None, None]
    bin_index = (
        np.arange(quarters, dtype=np.int64)[None, :, None] * per_quarter
        + np.arange(per_quarter, dtype=np.int64)[None, None, :]
    )
    phase_angle = (sample_index * bin_index % window_len).astype(np.float32) * np.float32(
        2.0 * math.pi / window_len
    )
    table = np.stack([np.cos(phase_angle), -np.sin(phase_angle)], axis=2)
    return jnp.asarray(table.reshape(window_len, 2 * bin_count).astype(jnp.bfloat16))


def band_matrix(bin_count, smooth_len):
    bin_index = jnp.arange(bin_count, dtype=jnp.int32)
    offsets = (bin_index[:, None] - bin_index[None, :]) % bin_count
    half_span = smooth_len // 2
    inside = (offsets < half_span) | (offsets >= bin_count - half_span)
    return inside.astype(jnp.float32)


ROWS = 32


def corr_kernel(order_ref, blk_ref, bound_ref, part_ref, own_ref, out_hbm, scr, wide, sem):
    h = pl.program_id(0)
    n_half, n_win, rows_all, freq = part_ref.shape
    n_pairs = order_ref.shape[0]
    n_top = out_hbm.shape[1]
    half = rows_all // 2
    chunk = min(ROWS, half)

    def one(i, carry):
        slot = i % 2
        p = order_ref[i]
        s = p // n_top
        k = p % n_top
        b = blk_ref[i] - h * n_half

        @pl.when(i >= 2)
        def _():
            pltpu.make_async_copy(scr.at[slot], out_hbm.at[0, 0], sem.at[slot]).wait()

        for c0 in range(0, half, chunk):
            real_sum = jnp.zeros((chunk, freq), jnp.float32)
            imag_sum = jnp.zeros((chunk, freq), jnp.float32)
            for w in range(n_win):
                par_re = part_ref[b, w, c0 : c0 + chunk, :].astype(jnp.float32)
                par_im = part_ref[b, w, half + c0 : half + c0 + chunk, :].astype(jnp.float32)
                sig_re = own_ref[w, pl.ds(s, 1), :]
                sig_im = own_ref[w, pl.ds(half + s, 1), :]
                real_sum = real_sum + par_re * sig_re + par_im * sig_im
                imag_sum = imag_sum + par_re * sig_im - par_im * sig_re
            wide[pl.ds(2 * c0, chunk, stride=2), :] = real_sum
            wide[pl.ds(2 * c0 + 1, chunk, stride=2), :] = imag_sum
        scr[slot] = wide[...].astype(scr.dtype)
        pltpu.make_async_copy(scr.at[slot], out_hbm.at[s, k], sem.at[slot]).start()
        return carry

    lax.fori_loop(bound_ref[h], bound_ref[h + 1], one, 0)

    @pl.when(h == pl.num_programs(0) - 1)
    def _():
        for back in range(min(2, n_pairs)):
            last = n_pairs - 1 - back
            pltpu.make_async_copy(scr.at[last % 2], out_hbm.at[0, 0], sem.at[last % 2]).wait()


def correlate(owners, part, own, out_shape):
    n_blocks, n_win, rows, freq = part.shape
    n_half = n_blocks // 2
    late = (owners >= n_half).astype(jnp.int32)
    order = jnp.argsort(late, stable=True).astype(jnp.int32)
    blk = owners[order].astype(jnp.int32)
    n_early = owners.shape[0] - jnp.sum(late)
    bounds = jnp.stack([jnp.zeros((), jnp.int32), n_early.astype(jnp.int32), jnp.full((), owners.shape[0], jnp.int32)])
    grid_spec = pltpu.PrefetchScalarGridSpec(
        num_scalar_prefetch=3,
        grid=(2,),
        in_specs=[
            pl.BlockSpec((n_half, n_win, rows, freq), lambda h, *_: (h, 0, 0, 0)),
            pl.BlockSpec(own.shape, lambda h, *_: (0, 0, 0)),
        ],
        out_specs=pl.BlockSpec(memory_space=pl.ANY),
        scratch_shapes=[
            pltpu.VMEM((2, rows, freq), jnp.bfloat16),
            pltpu.VMEM((rows, freq), jnp.float32),
            pltpu.SemaphoreType.DMA((2,)),
        ],
    )
    return pl.pallas_call(
        corr_kernel,
        out_shape=jax.ShapeDtypeStruct(out_shape, jnp.bfloat16),
        grid_spec=grid_spec,
        compiler_params=pltpu.CompilerParams(
            dimension_semantics=("arbitrary",), vmem_limit_bytes=48 * 1024 * 1024
        ),
    )(order, blk, bounds, part, own)


def shards(records, band_taps, station_owners):
    relayed = lax.all_to_all(records, "tm", split_axis=0, concat_axis=1, tiled=True)
    station_count = relayed.shape[0]
    both_parts = toeplitz_both(band_taps)
    series = relayed.reshape(station_count * NW, WIN)
    halves = jnp.dot(series, both_parts, preferred_element_type=jnp.float32)
    halves = halves.reshape(station_count, NW, 2 * WIN)
    carried = jnp.concatenate(
        [jnp.zeros_like(halves[:, :1, WIN:]), halves[:, :-1, WIN:]], axis=1
    )
    filtered = (halves[:, :, :WIN] + carried).astype(jnp.bfloat16).reshape(-1, WIN)
    quarters = records.shape[0] // station_count
    per_quarter = FREQ // quarters
    spectrum = jnp.dot(
        filtered, transform_table(WIN, quarters), preferred_element_type=jnp.float32
    ).reshape(-1, quarters, 2, per_quarter)
    power_sum = (
        spectrum[:, :, 0] * spectrum[:, :, 0] + spectrum[:, :, 1] * spectrum[:, :, 1]
    ).reshape(-1, FREQ)
    smooth = (
        jnp.dot(
            power_sum,
            band_matrix(FREQ, SMOOTH),
            precision=lax.Precision.HIGHEST,
            preferred_element_type=jnp.float32,
        )
        / SMOOTH
    )
    whiten_scale = lax.rsqrt(smooth + 1e-05).reshape(-1, quarters, 1, per_quarter)
    whitened = (spectrum * whiten_scale).astype(jnp.bfloat16)
    whitened = whitened.reshape(station_count, NW, quarters, 2, per_quarter).transpose(
        2, 1, 3, 0, 4
    )
    contribution = lax.all_to_all(whitened, "tm", split_axis=0, concat_axis=3, tiled=True)
    own_count = contribution.shape[3]
    contribution = contribution.reshape(NW, own_count * 2, per_quarter)
    gathered = lax.all_gather(contribution, "sta", axis=0, tiled=False)
    own = contribution.astype(jnp.float32)
    out_shape = (own_count, station_owners.shape[1], own_count * 2, per_quarter)
    result = correlate(station_owners.reshape(-1), gathered, own, out_shape)
    return result.reshape(own_count, station_owners.shape[1], own_count, 2, per_quarter)


def solution(mesh):
    placed = (P("sta", "tm"), P(), P("sta", None))
    return jax.shard_map(
        shards,
        mesh=mesh,
        in_specs=placed,
        out_specs=P("sta", None, None, None, "tm"),
        check_vma=False,
    )
```

```python
import math

import jax
import numpy as np
import jax.numpy as jnp
from jax import lax
from jax.experimental import pallas as pl
from jax.experimental.pallas import tpu as pltpu
from jax.sharding import PartitionSpec as P

WIN = 1024
FREQ = 512
SMOOTH = 64
NW = 8
CORES = 2


def toeplitz_kernel(seed_ref, out_ref):
    rows = 128
    base = jnp.broadcast_to(seed_ref[...], (rows, seed_ref.shape[1]))
    for blk in range(out_ref.shape[0] // rows):
        rolled = pltpu.roll(base, blk * rows, 1, stride=1, stride_axis=0)
        out_ref[blk * rows : (blk + 1) * rows, :] = rolled.astype(out_ref.dtype)


def toeplitz_both(band_taps):
    taps_len = band_taps.shape[0]
    seed = jnp.concatenate(
        [band_taps.astype(jnp.float32), jnp.zeros((taps_len,), jnp.float32)]
    )[None, :]
    return pl.pallas_call(
        toeplitz_kernel,
        out_shape=jax.ShapeDtypeStruct((taps_len, 2 * taps_len), jnp.bfloat16),
    )(seed)


def transform_table(window_len, quarters):
    bin_count = window_len // 2
    per_quarter = bin_count // quarters
    sample_index = np.arange(window_len, dtype=np.int64)[:, None, None]
    bin_index = (
        np.arange(quarters, dtype=np.int64)[None, :, None] * per_quarter
        + np.arange(per_quarter, dtype=np.int64)[None, None, :]
    )
    phase_angle = (sample_index * bin_index % window_len).astype(np.float32) * np.float32(
        2.0 * math.pi / window_len
    )
    table = np.stack([np.cos(phase_angle), -np.sin(phase_angle)], axis=2)
    return jnp.asarray(table.reshape(window_len, 2 * bin_count).astype(jnp.bfloat16))


def band_matrix(bin_count, smooth_len):
    bin_index = jnp.arange(bin_count, dtype=jnp.int32)
    offsets = (bin_index[:, None] - bin_index[None, :]) % bin_count
    half_span = smooth_len // 2
    inside = (offsets < half_span) | (offsets >= bin_count - half_span)
    return inside.astype(jnp.float32)


ROWS = 32


def corr_kernel(order_ref, blk_ref, bound_ref, part_ref, own_ref, out_hbm, scr, wide, sem):
    h = pl.program_id(0)
    n_half, n_win, rows_all, freq = part_ref.shape
    n_pairs = order_ref.shape[0]
    n_top = out_hbm.shape[1]
    half = rows_all // 2
    chunk = min(ROWS, half)

    def one(i, carry):
        slot = i % 2
        p = order_ref[i]
        s = p // n_top
        k = p % n_top
        b = blk_ref[i] - h * n_half

        @pl.when(i >= 2)
        def _():
            pltpu.make_async_copy(scr.at[slot], out_hbm.at[0, 0], sem.at[slot]).wait()

        for c0 in range(0, half, chunk):
            real_sum = jnp.zeros((chunk, freq), jnp.float32)
            imag_sum = jnp.zeros((chunk, freq), jnp.float32)
            for w in range(n_win):
                par_re = part_ref[b, w, c0 : c0 + chunk, :].astype(jnp.float32)
                par_im = part_ref[b, w, half + c0 : half + c0 + chunk, :].astype(jnp.float32)
                sig_re = own_ref[w, pl.ds(s, 1), :]
                sig_im = own_ref[w, pl.ds(half + s, 1), :]
                real_sum = real_sum + par_re * sig_re + par_im * sig_im
                imag_sum = imag_sum + par_re * sig_im - par_im * sig_re
            wide[pl.ds(2 * c0, chunk, stride=2), :] = real_sum
            wide[pl.ds(2 * c0 + 1, chunk, stride=2), :] = imag_sum
        scr[slot] = wide[...].astype(scr.dtype)
        pltpu.make_async_copy(scr.at[slot], out_hbm.at[s, k], sem.at[slot]).start()
        return carry

    lax.fori_loop(bound_ref[h], bound_ref[h + 1], one, 0)

    @pl.when(h == pl.num_programs(0) - 1)
    def _():
        for back in range(min(2, n_pairs)):
            last = n_pairs - 1 - back
            pltpu.make_async_copy(scr.at[last % 2], out_hbm.at[0, 0], sem.at[last % 2]).wait()


def correlate(owners, part, own, out_shape, n_parts=4):
    n_blocks, n_win, rows, freq = part.shape
    n_half = n_blocks // n_parts
    part_of = (owners // n_half).astype(jnp.int32)
    order = jnp.argsort(part_of, stable=True).astype(jnp.int32)
    blk = owners[order].astype(jnp.int32)
    counts = jnp.sum(
        (part_of[None, :] == jnp.arange(n_parts, dtype=jnp.int32)[:, None]).astype(jnp.int32),
        axis=1,
    )
    bounds = jnp.concatenate([jnp.zeros((1,), jnp.int32), jnp.cumsum(counts).astype(jnp.int32)])
    grid_spec = pltpu.PrefetchScalarGridSpec(
        num_scalar_prefetch=3,
        grid=(n_parts,),
        in_specs=[
            pl.BlockSpec((n_half, n_win, rows, freq), lambda h, *_: (h, 0, 0, 0)),
            pl.BlockSpec(own.shape, lambda h, *_: (0, 0, 0)),
        ],
        out_specs=pl.BlockSpec(memory_space=pl.ANY),
        scratch_shapes=[
            pltpu.VMEM((2, rows, freq), jnp.bfloat16),
            pltpu.VMEM((rows, freq), jnp.float32),
            pltpu.SemaphoreType.DMA((2,)),
        ],
    )
    return pl.pallas_call(
        corr_kernel,
        out_shape=jax.ShapeDtypeStruct(out_shape, jnp.bfloat16),
        grid_spec=grid_spec,
        compiler_params=pltpu.CompilerParams(
            dimension_semantics=("arbitrary",), vmem_limit_bytes=48 * 1024 * 1024
        ),
    )(order, blk, bounds, part, own)


def shards(records, band_taps, station_owners):
    relayed = lax.all_to_all(records, "tm", split_axis=0, concat_axis=1, tiled=True)
    station_count = relayed.shape[0]
    both_parts = toeplitz_both(band_taps)
    series = relayed.reshape(station_count * NW, WIN)
    halves = jnp.dot(series, both_parts, preferred_element_type=jnp.float32)
    halves = halves.reshape(station_count, NW, 2 * WIN)
    carried = jnp.concatenate(
        [jnp.zeros_like(halves[:, :1, WIN:]), halves[:, :-1, WIN:]], axis=1
    )
    filtered = (halves[:, :, :WIN] + carried).astype(jnp.bfloat16).reshape(-1, WIN)
    quarters = records.shape[0] // station_count
    per_quarter = FREQ // quarters
    spectrum = jnp.dot(
        filtered, transform_table(WIN, quarters), preferred_element_type=jnp.float32
    ).reshape(-1, quarters, 2, per_quarter)
    power_sum = (
        spectrum[:, :, 0] * spectrum[:, :, 0] + spectrum[:, :, 1] * spectrum[:, :, 1]
    ).reshape(-1, FREQ)
    smooth = (
        jnp.dot(
            power_sum,
            band_matrix(FREQ, SMOOTH),
            precision=lax.Precision.HIGHEST,
            preferred_element_type=jnp.float32,
        )
        / SMOOTH
    )
    whiten_scale = lax.rsqrt(smooth + 1e-05).reshape(-1, quarters, 1, per_quarter)
    whitened = (spectrum * whiten_scale).astype(jnp.bfloat16)
    whitened = whitened.reshape(station_count, NW, quarters, 2, per_quarter).transpose(
        2, 1, 3, 0, 4
    )
    contribution = lax.all_to_all(whitened, "tm", split_axis=0, concat_axis=3, tiled=True)
    own_count = contribution.shape[3]
    contribution = contribution.reshape(NW, own_count * 2, per_quarter)
    gathered = lax.all_gather(contribution, "sta", axis=0, tiled=False)
    own = contribution.astype(jnp.float32)
    out_shape = (own_count, station_owners.shape[1], own_count * 2, per_quarter)
    result = correlate(station_owners.reshape(-1), gathered, own, out_shape)
    return result.reshape(own_count, station_owners.shape[1], own_count, 2, per_quarter)


def solution(mesh):
    placed = (P("sta", "tm"), P(), P("sta", None))
    return jax.shard_map(
        shards,
        mesh=mesh,
        in_specs=placed,
        out_specs=P("sta", None, None, None, "tm"),
        check_vma=False,
    )
```

```python
import math

import jax
import numpy as np
import jax.numpy as jnp
from jax import lax
from jax.experimental import pallas as pl
from jax.experimental.pallas import tpu as pltpu
from jax.sharding import PartitionSpec as P

WIN = 1024
FREQ = 512
SMOOTH = 64
NW = 8
CORES = 2


def toeplitz_kernel(seed_ref, out_ref):
    rows = 128
    base = jnp.broadcast_to(seed_ref[...], (rows, seed_ref.shape[1]))
    for blk in range(out_ref.shape[0] // rows):
        rolled = pltpu.roll(base, blk * rows, 1, stride=1, stride_axis=0)
        out_ref[blk * rows : (blk + 1) * rows, :] = rolled.astype(out_ref.dtype)


def toeplitz_both(band_taps):
    taps_len = band_taps.shape[0]
    seed = jnp.concatenate(
        [band_taps.astype(jnp.float32), jnp.zeros((taps_len,), jnp.float32)]
    )[None, :]
    return pl.pallas_call(
        toeplitz_kernel,
        out_shape=jax.ShapeDtypeStruct((taps_len, 2 * taps_len), jnp.bfloat16),
    )(seed)


def transform_table(window_len, quarters):
    bin_count = window_len // 2
    per_quarter = bin_count // quarters
    sample_index = np.arange(window_len, dtype=np.int64)[:, None, None]
    bin_index = (
        np.arange(quarters, dtype=np.int64)[None, :, None] * per_quarter
        + np.arange(per_quarter, dtype=np.int64)[None, None, :]
    )
    phase_angle = (sample_index * bin_index % window_len).astype(np.float32) * np.float32(
        2.0 * math.pi / window_len
    )
    table = np.stack([np.cos(phase_angle), -np.sin(phase_angle)], axis=2)
    return jnp.asarray(table.reshape(window_len, 2 * bin_count).astype(jnp.bfloat16))


def band_matrix(bin_count, smooth_len):
    bin_index = jnp.arange(bin_count, dtype=jnp.int32)
    offsets = (bin_index[:, None] - bin_index[None, :]) % bin_count
    half_span = smooth_len // 2
    inside = (offsets < half_span) | (offsets >= bin_count - half_span)
    return inside.astype(jnp.float32)


ROWS = 32


def corr_kernel(order_ref, blk_ref, bound_ref, part_ref, own_ref, out_hbm, scr, wide, sem):
    h = pl.program_id(0)
    n_half, n_win, rows_all, freq = part_ref.shape
    n_pairs = order_ref.shape[0]
    n_top = out_hbm.shape[1]
    half = rows_all // 2
    chunk = min(ROWS, half)

    def one(i, carry):
        slot = i % 2
        p = order_ref[i]
        s = p // n_top
        k = p % n_top
        b = blk_ref[i] - h * n_half

        @pl.when(i >= 2)
        def _():
            pltpu.make_async_copy(scr.at[slot], out_hbm.at[0, 0], sem.at[slot]).wait()

        for c0 in range(0, half, chunk):
            real_sum = jnp.zeros((chunk, freq), jnp.float32)
            imag_sum = jnp.zeros((chunk, freq), jnp.float32)
            for w in range(n_win):
                par_re = part_ref[b, w, c0 : c0 + chunk, :].astype(jnp.float32)
                par_im = part_ref[b, w, half + c0 : half + c0 + chunk, :].astype(jnp.float32)
                sig_re = own_ref[w, pl.ds(s, 1), :]
                sig_im = own_ref[w, pl.ds(half + s, 1), :]
                real_sum = real_sum + par_re * sig_re + par_im * sig_im
                imag_sum = imag_sum + par_re * sig_im - par_im * sig_re
            wide[pl.ds(2 * c0, chunk, stride=2), :] = real_sum
            wide[pl.ds(2 * c0 + 1, chunk, stride=2), :] = imag_sum
        scr[slot] = wide[...].astype(scr.dtype)
        pltpu.make_async_copy(scr.at[slot], out_hbm.at[s, k], sem.at[slot]).start()
        return carry

    lax.fori_loop(bound_ref[h], bound_ref[h + 1], one, 0)

    @pl.when(h == pl.num_programs(0) - 1)
    def _():
        for back in range(min(2, n_pairs)):
            last = n_pairs - 1 - back
            pltpu.make_async_copy(scr.at[last % 2], out_hbm.at[0, 0], sem.at[last % 2]).wait()


def correlate(owners, part, own, out_shape, n_parts=8):
    n_blocks, n_win, rows, freq = part.shape
    n_half = n_blocks // n_parts
    part_of = (owners // n_half).astype(jnp.int32)
    order = jnp.argsort(part_of, stable=True).astype(jnp.int32)
    blk = owners[order].astype(jnp.int32)
    counts = jnp.sum(
        (part_of[None, :] == jnp.arange(n_parts, dtype=jnp.int32)[:, None]).astype(jnp.int32),
        axis=1,
    )
    bounds = jnp.concatenate([jnp.zeros((1,), jnp.int32), jnp.cumsum(counts).astype(jnp.int32)])
    grid_spec = pltpu.PrefetchScalarGridSpec(
        num_scalar_prefetch=3,
        grid=(n_parts,),
        in_specs=[
            pl.BlockSpec((n_half, n_win, rows, freq), lambda h, *_: (h, 0, 0, 0)),
            pl.BlockSpec(own.shape, lambda h, *_: (0, 0, 0)),
        ],
        out_specs=pl.BlockSpec(memory_space=pl.ANY),
        scratch_shapes=[
            pltpu.VMEM((2, rows, freq), jnp.bfloat16),
            pltpu.VMEM((rows, freq), jnp.float32),
            pltpu.SemaphoreType.DMA((2,)),
        ],
    )
    return pl.pallas_call(
        corr_kernel,
        out_shape=jax.ShapeDtypeStruct(out_shape, jnp.bfloat16),
        grid_spec=grid_spec,
        compiler_params=pltpu.CompilerParams(
            dimension_semantics=("arbitrary",), vmem_limit_bytes=48 * 1024 * 1024
        ),
    )(order, blk, bounds, part, own)


def shards(records, band_taps, station_owners):
    relayed = lax.all_to_all(records, "tm", split_axis=0, concat_axis=1, tiled=True)
    station_count = relayed.shape[0]
    both_parts = toeplitz_both(band_taps)
    series = relayed.reshape(station_count * NW, WIN)
    halves = jnp.dot(series, both_parts, preferred_element_type=jnp.float32)
    halves = halves.reshape(station_count, NW, 2 * WIN)
    carried = jnp.concatenate(
        [jnp.zeros_like(halves[:, :1, WIN:]), halves[:, :-1, WIN:]], axis=1
    )
    filtered = (halves[:, :, :WIN] + carried).astype(jnp.bfloat16).reshape(-1, WIN)
    quarters = records.shape[0] // station_count
    per_quarter = FREQ // quarters
    spectrum = jnp.dot(
        filtered, transform_table(WIN, quarters), preferred_element_type=jnp.float32
    ).reshape(-1, quarters, 2, per_quarter)
    power_sum = (
        spectrum[:, :, 0] * spectrum[:, :, 0] + spectrum[:, :, 1] * spectrum[:, :, 1]
    ).reshape(-1, FREQ)
    smooth = (
        jnp.dot(
            power_sum,
            band_matrix(FREQ, SMOOTH),
            precision=lax.Precision.HIGHEST,
            preferred_element_type=jnp.float32,
        )
        / SMOOTH
    )
    whiten_scale = lax.rsqrt(smooth + 1e-05).reshape(-1, quarters, 1, per_quarter)
    whitened = (spectrum * whiten_scale).astype(jnp.bfloat16)
    whitened = whitened.reshape(station_count, NW, quarters, 2, per_quarter).transpose(
        2, 1, 3, 0, 4
    )
    contribution = lax.all_to_all(whitened, "tm", split_axis=0, concat_axis=3, tiled=True)
    own_count = contribution.shape[3]
    contribution = contribution.reshape(NW, own_count * 2, per_quarter)
    gathered = lax.all_gather(contribution, "sta", axis=0, tiled=False)
    own = contribution.astype(jnp.float32)
    out_shape = (own_count, station_owners.shape[1], own_count * 2, per_quarter)
    result = correlate(station_owners.reshape(-1), gathered, own, out_shape)
    return result.reshape(own_count, station_owners.shape[1], own_count, 2, per_quarter)


def solution(mesh):
    placed = (P("sta", "tm"), P(), P("sta", None))
    return jax.shard_map(
        shards,
        mesh=mesh,
        in_specs=placed,
        out_specs=P("sta", None, None, None, "tm"),
        check_vma=False,
    )
```

```python
import math

import jax
import numpy as np
import jax.numpy as jnp
from jax import lax
from jax.experimental import pallas as pl
from jax.experimental.pallas import tpu as pltpu
from jax.sharding import PartitionSpec as P

WIN = 1024
FREQ = 512
SMOOTH = 64
NW = 8
CORES = 2


def toeplitz_kernel(seed_ref, out_ref):
    rows = 128
    base = jnp.broadcast_to(seed_ref[...], (rows, seed_ref.shape[1]))
    for blk in range(out_ref.shape[0] // rows):
        rolled = pltpu.roll(base, blk * rows, 1, stride=1, stride_axis=0)
        out_ref[blk * rows : (blk + 1) * rows, :] = rolled.astype(out_ref.dtype)


def toeplitz_both(band_taps):
    taps_len = band_taps.shape[0]
    seed = jnp.concatenate(
        [band_taps.astype(jnp.float32), jnp.zeros((taps_len,), jnp.float32)]
    )[None, :]
    return pl.pallas_call(
        toeplitz_kernel,
        out_shape=jax.ShapeDtypeStruct((taps_len, 2 * taps_len), jnp.bfloat16),
    )(seed)


def transform_table(window_len, quarters):
    bin_count = window_len // 2
    per_quarter = bin_count // quarters
    sample_index = np.arange(window_len, dtype=np.int64)[:, None, None]
    bin_index = (
        np.arange(quarters, dtype=np.int64)[None, :, None] * per_quarter
        + np.arange(per_quarter, dtype=np.int64)[None, None, :]
    )
    phase_angle = (sample_index * bin_index % window_len).astype(np.float32) * np.float32(
        2.0 * math.pi / window_len
    )
    table = np.stack([np.cos(phase_angle), -np.sin(phase_angle)], axis=2)
    return jnp.asarray(table.reshape(window_len, 2 * bin_count).astype(jnp.bfloat16))


def band_matrix(bin_count, smooth_len):
    bin_index = jnp.arange(bin_count, dtype=jnp.int32)
    offsets = (bin_index[:, None] - bin_index[None, :]) % bin_count
    half_span = smooth_len // 2
    inside = (offsets < half_span) | (offsets >= bin_count - half_span)
    return inside.astype(jnp.float32)


ROWS = 32


def corr_kernel(order_ref, blk_ref, bound_ref, part_ref, own_ref, out_hbm, scr, wide, sem):
    h = pl.program_id(0)
    n_half, n_win, rows_all, freq = part_ref.shape
    n_pairs = order_ref.shape[0]
    n_top = out_hbm.shape[1]
    half = rows_all // 2
    chunk = min(ROWS, half)

    def one(i, carry):
        slot = i % 2
        p = order_ref[i]
        s = p // n_top
        k = p % n_top
        b = blk_ref[i] - h * n_half

        @pl.when(i >= 2)
        def _():
            pltpu.make_async_copy(scr.at[slot], out_hbm.at[0, 0], sem.at[slot]).wait()

        for c0 in range(0, half, chunk):
            real_sum = jnp.zeros((chunk, freq), jnp.float32)
            imag_sum = jnp.zeros((chunk, freq), jnp.float32)
            for w in range(n_win):
                par_re = part_ref[b, w, c0 : c0 + chunk, :].astype(jnp.float32)
                par_im = part_ref[b, w, half + c0 : half + c0 + chunk, :].astype(jnp.float32)
                sig_re = own_ref[w, pl.ds(s, 1), :]
                sig_im = own_ref[w, pl.ds(half + s, 1), :]
                real_sum = real_sum + par_re * sig_re + par_im * sig_im
                imag_sum = imag_sum + par_re * sig_im - par_im * sig_re
            wide[pl.ds(2 * c0, chunk, stride=2), :] = real_sum
            wide[pl.ds(2 * c0 + 1, chunk, stride=2), :] = imag_sum
        scr[slot] = wide[...].astype(scr.dtype)
        pltpu.make_async_copy(scr.at[slot], out_hbm.at[s, k], sem.at[slot]).start()
        return carry

    lax.fori_loop(bound_ref[h], bound_ref[h + 1], one, 0)

    @pl.when(h == pl.num_programs(0) - 1)
    def _():
        for back in range(min(2, n_pairs)):
            last = n_pairs - 1 - back
            pltpu.make_async_copy(scr.at[last % 2], out_hbm.at[0, 0], sem.at[last % 2]).wait()


def correlate(owners, part, own, out_shape, n_parts=16):
    n_blocks, n_win, rows, freq = part.shape
    n_half = n_blocks // n_parts
    part_of = (owners // n_half).astype(jnp.int32)
    order = jnp.argsort(part_of, stable=True).astype(jnp.int32)
    blk = owners[order].astype(jnp.int32)
    counts = jnp.sum(
        (part_of[None, :] == jnp.arange(n_parts, dtype=jnp.int32)[:, None]).astype(jnp.int32),
        axis=1,
    )
    bounds = jnp.concatenate([jnp.zeros((1,), jnp.int32), jnp.cumsum(counts).astype(jnp.int32)])
    grid_spec = pltpu.PrefetchScalarGridSpec(
        num_scalar_prefetch=3,
        grid=(n_parts,),
        in_specs=[
            pl.BlockSpec((n_half, n_win, rows, freq), lambda h, *_: (h, 0, 0, 0)),
            pl.BlockSpec(own.shape, lambda h, *_: (0, 0, 0)),
        ],
        out_specs=pl.BlockSpec(memory_space=pl.ANY),
        scratch_shapes=[
            pltpu.VMEM((2, rows, freq), jnp.bfloat16),
            pltpu.VMEM((rows, freq), jnp.float32),
            pltpu.SemaphoreType.DMA((2,)),
        ],
    )
    return pl.pallas_call(
        corr_kernel,
        out_shape=jax.ShapeDtypeStruct(out_shape, jnp.bfloat16),
        grid_spec=grid_spec,
        compiler_params=pltpu.CompilerParams(
            dimension_semantics=("arbitrary",), vmem_limit_bytes=48 * 1024 * 1024
        ),
    )(order, blk, bounds, part, own)


def shards(records, band_taps, station_owners):
    relayed = lax.all_to_all(records, "tm", split_axis=0, concat_axis=1, tiled=True)
    station_count = relayed.shape[0]
    both_parts = toeplitz_both(band_taps)
    series = relayed.reshape(station_count * NW, WIN)
    halves = jnp.dot(series, both_parts, preferred_element_type=jnp.float32)
    halves = halves.reshape(station_count, NW, 2 * WIN)
    carried = jnp.concatenate(
        [jnp.zeros_like(halves[:, :1, WIN:]), halves[:, :-1, WIN:]], axis=1
    )
    filtered = (halves[:, :, :WIN] + carried).astype(jnp.bfloat16).reshape(-1, WIN)
    quarters = records.shape[0] // station_count
    per_quarter = FREQ // quarters
    spectrum = jnp.dot(
        filtered, transform_table(WIN, quarters), preferred_element_type=jnp.float32
    ).reshape(-1, quarters, 2, per_quarter)
    power_sum = (
        spectrum[:, :, 0] * spectrum[:, :, 0] + spectrum[:, :, 1] * spectrum[:, :, 1]
    ).reshape(-1, FREQ)
    smooth = (
        jnp.dot(
            power_sum,
            band_matrix(FREQ, SMOOTH),
            precision=lax.Precision.HIGHEST,
            preferred_element_type=jnp.float32,
        )
        / SMOOTH
    )
    whiten_scale = lax.rsqrt(smooth + 1e-05).reshape(-1, quarters, 1, per_quarter)
    whitened = (spectrum * whiten_scale).astype(jnp.bfloat16)
    whitened = whitened.reshape(station_count, NW, quarters, 2, per_quarter).transpose(
        2, 1, 3, 0, 4
    )
    contribution = lax.all_to_all(whitened, "tm", split_axis=0, concat_axis=3, tiled=True)
    own_count = contribution.shape[3]
    contribution = contribution.reshape(NW, own_count * 2, per_quarter)
    gathered = lax.all_gather(contribution, "sta", axis=0, tiled=False)
    own = contribution.astype(jnp.float32)
    out_shape = (own_count, station_owners.shape[1], own_count * 2, per_quarter)
    result = correlate(station_owners.reshape(-1), gathered, own, out_shape)
    return result.reshape(own_count, station_owners.shape[1], own_count, 2, per_quarter)


def solution(mesh):
    placed = (P("sta", "tm"), P(), P("sta", None))
    return jax.shard_map(
        shards,
        mesh=mesh,
        in_specs=placed,
        out_specs=P("sta", None, None, None, "tm"),
        check_vma=False,
    )
```

```python
import math

import jax
import numpy as np
import jax.numpy as jnp
from jax import lax
from jax.experimental import pallas as pl
from jax.experimental.pallas import tpu as pltpu
from jax.sharding import PartitionSpec as P

WIN = 1024
FREQ = 512
SMOOTH = 64
NW = 8
CORES = 2


def toeplitz_kernel(seed_ref, out_ref):
    rows = 128
    base = jnp.broadcast_to(seed_ref[...], (rows, seed_ref.shape[1]))
    for blk in range(out_ref.shape[0] // rows):
        rolled = pltpu.roll(base, blk * rows, 1, stride=1, stride_axis=0)
        out_ref[blk * rows : (blk + 1) * rows, :] = rolled.astype(out_ref.dtype)


def toeplitz_both(band_taps):
    taps_len = band_taps.shape[0]
    seed = jnp.concatenate(
        [band_taps.astype(jnp.float32), jnp.zeros((taps_len,), jnp.float32)]
    )[None, :]
    return pl.pallas_call(
        toeplitz_kernel,
        out_shape=jax.ShapeDtypeStruct((taps_len, 2 * taps_len), jnp.bfloat16),
    )(seed)


def transform_table(window_len, quarters):
    bin_count = window_len // 2
    per_quarter = bin_count // quarters
    sample_index = np.arange(window_len, dtype=np.int64)[:, None, None]
    bin_index = (
        np.arange(quarters, dtype=np.int64)[None, :, None] * per_quarter
        + np.arange(per_quarter, dtype=np.int64)[None, None, :]
    )
    phase_angle = (sample_index * bin_index % window_len).astype(np.float32) * np.float32(
        2.0 * math.pi / window_len
    )
    table = np.stack([np.cos(phase_angle), -np.sin(phase_angle)], axis=2)
    return jnp.asarray(table.reshape(window_len, 2 * bin_count).astype(jnp.bfloat16))


def band_matrix(bin_count, smooth_len):
    bin_index = jnp.arange(bin_count, dtype=jnp.int32)
    offsets = (bin_index[:, None] - bin_index[None, :]) % bin_count
    half_span = smooth_len // 2
    inside = (offsets < half_span) | (offsets >= bin_count - half_span)
    return inside.astype(jnp.float32)


ROWS = 32


def corr_kernel(order_ref, blk_ref, bound_ref, part_ref, own_ref, out_hbm, scr, wide, sem):
    h = pl.program_id(0)
    n_half, n_src, n_win, rows, freq = part_ref.shape
    n_pairs = order_ref.shape[0]
    n_top = out_hbm.shape[1]
    per = rows // 2

    def one(i, carry):
        slot = i % 2
        p = order_ref[i]
        s = p // n_top
        k = p % n_top
        b = blk_ref[i] - h * n_half

        @pl.when(i >= 2)
        def _():
            pltpu.make_async_copy(scr.at[slot], out_hbm.at[0, 0], sem.at[slot]).wait()

        for src in range(n_src):
            real_sum = jnp.zeros((per, freq), jnp.float32)
            imag_sum = jnp.zeros((per, freq), jnp.float32)
            for w in range(n_win):
                par_re = part_ref[b, src, w, 0:per, :].astype(jnp.float32)
                par_im = part_ref[b, src, w, per:rows, :].astype(jnp.float32)
                sig_re = own_ref[s // per, w, pl.ds(s % per, 1), :]
                sig_im = own_ref[s // per, w, pl.ds(per + s % per, 1), :]
                real_sum = real_sum + par_re * sig_re + par_im * sig_im
                imag_sum = imag_sum + par_re * sig_im - par_im * sig_re
            wide[pl.ds(2 * src * per, per, stride=2), :] = real_sum
            wide[pl.ds(2 * src * per + 1, per, stride=2), :] = imag_sum
        scr[slot] = wide[...].astype(scr.dtype)
        pltpu.make_async_copy(scr.at[slot], out_hbm.at[s, k], sem.at[slot]).start()
        return carry

    lax.fori_loop(bound_ref[h], bound_ref[h + 1], one, 0)

    @pl.when(h == pl.num_programs(0) - 1)
    def _():
        for back in range(min(2, n_pairs)):
            last = n_pairs - 1 - back
            pltpu.make_async_copy(scr.at[last % 2], out_hbm.at[0, 0], sem.at[last % 2]).wait()


def correlate(owners, part, own, out_shape, n_parts=16):
    n_blocks, n_src, n_win, rows, freq = part.shape
    n_half = n_blocks // n_parts
    part_of = (owners // n_half).astype(jnp.int32)
    order = jnp.argsort(part_of, stable=True).astype(jnp.int32)
    blk = owners[order].astype(jnp.int32)
    counts = jnp.sum(
        (part_of[None, :] == jnp.arange(n_parts, dtype=jnp.int32)[:, None]).astype(jnp.int32),
        axis=1,
    )
    bounds = jnp.concatenate([jnp.zeros((1,), jnp.int32), jnp.cumsum(counts).astype(jnp.int32)])
    grid_spec = pltpu.PrefetchScalarGridSpec(
        num_scalar_prefetch=3,
        grid=(n_parts,),
        in_specs=[
            pl.BlockSpec((n_half, n_src, n_win, rows, freq), lambda h, *_: (h, 0, 0, 0, 0)),
            pl.BlockSpec(own.shape, lambda h, *_: (0, 0, 0, 0)),
        ],
        out_specs=pl.BlockSpec(memory_space=pl.ANY),
        scratch_shapes=[
            pltpu.VMEM((2, n_src * rows, freq), jnp.bfloat16),
            pltpu.VMEM((n_src * rows, freq), jnp.float32),
            pltpu.SemaphoreType.DMA((2,)),
        ],
    )
    return pl.pallas_call(
        corr_kernel,
        out_shape=jax.ShapeDtypeStruct(out_shape, jnp.bfloat16),
        grid_spec=grid_spec,
        compiler_params=pltpu.CompilerParams(
            dimension_semantics=("arbitrary",), vmem_limit_bytes=48 * 1024 * 1024
        ),
    )(order, blk, bounds, part, own)


def shards(records, band_taps, station_owners):
    relayed = lax.all_to_all(records, "tm", split_axis=0, concat_axis=1, tiled=True)
    station_count = relayed.shape[0]
    both_parts = toeplitz_both(band_taps)
    series = relayed.reshape(station_count * NW, WIN)
    halves = jnp.dot(series, both_parts, preferred_element_type=jnp.float32)
    halves = halves.reshape(station_count, NW, 2 * WIN)
    carried = jnp.concatenate(
        [jnp.zeros_like(halves[:, :1, WIN:]), halves[:, :-1, WIN:]], axis=1
    )
    filtered = (halves[:, :, :WIN] + carried).astype(jnp.bfloat16).reshape(-1, WIN)
    quarters = records.shape[0] // station_count
    per_quarter = FREQ // quarters
    spectrum = jnp.dot(
        filtered, transform_table(WIN, quarters), preferred_element_type=jnp.float32
    ).reshape(-1, quarters, 2, per_quarter)
    power_sum = (
        spectrum[:, :, 0] * spectrum[:, :, 0] + spectrum[:, :, 1] * spectrum[:, :, 1]
    ).reshape(-1, FREQ)
    smooth = (
        jnp.dot(
            power_sum,
            band_matrix(FREQ, SMOOTH),
            precision=lax.Precision.HIGHEST,
            preferred_element_type=jnp.float32,
        )
        / SMOOTH
    )
    whiten_scale = lax.rsqrt(smooth + 1e-05).reshape(-1, quarters, 1, per_quarter)
    whitened = (spectrum * whiten_scale).astype(jnp.bfloat16)
    whitened = whitened.reshape(station_count, NW, quarters, 2, per_quarter).transpose(
        2, 1, 3, 0, 4
    )
    contribution = lax.all_to_all(whitened, "tm", split_axis=0, concat_axis=0, tiled=True)
    own_count = quarters * station_count
    contribution = contribution.reshape(quarters, NW, 2 * station_count, per_quarter)
    gathered = lax.all_gather(contribution, "sta", axis=0, tiled=False)
    own = contribution.astype(jnp.float32)
    out_shape = (own_count, station_owners.shape[1], own_count * 2, per_quarter)
    result = correlate(station_owners.reshape(-1), gathered, own, out_shape)
    return result.reshape(own_count, station_owners.shape[1], own_count, 2, per_quarter)


def solution(mesh):
    placed = (P("sta", "tm"), P(), P("sta", None))
    return jax.shard_map(
        shards,
        mesh=mesh,
        in_specs=placed,
        out_specs=P("sta", None, None, None, "tm"),
        check_vma=False,
    )
```
